32 devices in a mesh: own: 4 (over z), rep: 8 (over y, x, core).
Axes of the slice: x: 2, y: 2, z: 4, core: 2. Of those that a mesh axis runs over, the one named last changes fastest.
Arguments:
- amplitudes: bfloat16 [1024, 16384], P('own', 'rep'), may hold values from -6 to 6
- integrals: bfloat16 [2048, 128, 128], P(('own', 'rep')), may hold values from -0.125 to 0.125
- ab_list: int32 [32, 32, 2], P(('own', 'rep')), may hold values from 0 to 15, as said below
- cd_list: int32 [32, 32, 2], P(('own', 'rep')), may hold values from 0 to 15
- live_count: int32 [32, 32], P(('own', 'rep')), may hold values from 0 to 2, as said below
Outputs:
- ladder: float32 [1024, 8192], P('rep', 'own')
The draws below stay inside these ranges and needn't reach their ends.
Inputs may be any that keep to these rules, and one draw needn't show every extreme that they name: live_count[d, s] is how many of the 2 slots from source s to destination d hold a tile; the rest are ignored; every device fills all its slots to itself. For one destination d, no two slots (of any sources) have the same pair (ab_list[d, s, k], cd_list[d, s, k]).
All inputs are finite; a program needn't handle non-finite values.
Results may differ from the reference program's by a relative error of at most 0.0003.
Values may be sent and summed in bfloat16 or wider, within the bound.
No kernel may reach another device: no remote copies, remote signals or barrier semaphores. Data moves between devices by JAX's collectives and lax.ppermute only.
A program may use at most 128 MiB of HBM per device.

```python
import jax
import jax.numpy as jnp
from jax import lax

TILE = 128
OP = 1024
AB_DEV = 16
CD_DEV = 16
SLOTS = 2
CD_TILES = 128
N_OWN = 4
N_REP = 8
DEVICES = 32


def draw_live_count(key, part):
    base = jax.random.randint(key, (DEVICES, DEVICES), 0, SLOTS + 1)
    diagonal = jnp.arange(DEVICES)[:, None] == jnp.arange(DEVICES)[None, :]
    return jnp.where(diagonal, SLOTS, base).astype(jnp.int32)


def cell_table(key):
    keys = jax.random.split(jax.random.fold_in(key, 7), DEVICES)
    cells = jax.vmap(lambda one: jax.random.permutation(one, AB_DEV * CD_DEV)[:DEVICES * SLOTS])(keys)
    return cells.reshape(DEVICES, DEVICES, SLOTS).astype(jnp.int32)


def draw_ab_list(key, part):
    return (cell_table(key) // CD_DEV).astype(jnp.int32)


def draw_cd_list(key, part):
    return (cell_table(key) % CD_DEV).astype(jnp.int32)


def level_of(stream_key, dims, shards, smallest, top_value):
    def one(dim, blocks):
        heights = jax.random.uniform(jax.random.fold_in(jax.random.fold_in(stream_key, 6), dim), (blocks,), jnp.float32, smallest / len(shards), top_value / len(shards))
        return jnp.repeat(jnp.exp(heights), dims[dim] // blocks).reshape((-1,) + (1,) * (len(dims) - dim - 1))

    level = one(*shards[0])
    for cut in shards[1:]:
        level = level * one(*cut)
    return level


def bell_draw(rng, dims, scale, bound, cuts=(), held_as=jnp.bfloat16):
    entries = jax.random.normal(rng, dims, jnp.float32) * scale
    if len(cuts) > 0:
        entries = level_of(rng, dims, cuts, -0.22, 0.18) * entries
    return jnp.clip(entries, min=-bound, max=bound).astype(held_as)


def setup_inputs(seed: int = 0) -> dict:
    arg_keys = jax.random.split(jax.random.key(seed), 6)
    return {
        "amplitudes": bell_draw(arg_keys[0], (OP, CD_TILES * TILE), 1.0, 6.0, ((0, 4), (1, 8))),
        "integrals": bell_draw(arg_keys[1], (DEVICES * DEVICES * SLOTS, TILE, TILE), (TILE * N_REP * DEVICES * SLOTS // (2 * AB_DEV)) ** -0.5, 0.125, ((0, 32),)),
        "ab_list": draw_ab_list(jax.random.fold_in(arg_keys[5], 71), 0),
        "cd_list": draw_cd_list(jax.random.fold_in(arg_keys[5], 71), 0),
        "live_count": draw_live_count(jax.random.fold_in(arg_keys[5], 71), 0),
    }


def reference(amplitudes, integrals, ab_list, cd_list, live_count):
    all_tiles = integrals.reshape(DEVICES, DEVICES, SLOTS, TILE, TILE)
    slot_index = jnp.arange(SLOTS, dtype=jnp.int32)

    def owner_block(owner):
        def add_rep(rep_idx, running):
            dest = (owner * N_REP + rep_idx).astype(jnp.int32)
            received = lax.dynamic_index_in_dim(all_tiles, dest, 1, False).reshape(DEVICES * SLOTS, TILE, TILE)
            ab_ids = lax.dynamic_index_in_dim(ab_list, dest, 0, False).reshape(-1)
            cd_ids = lax.dynamic_index_in_dim(cd_list, dest, 0, False).reshape(-1)
            counts = lax.dynamic_index_in_dim(live_count, dest, 0, False)
            live_mask = (slot_index[None, :] < counts[:, None]).reshape(-1)
            masked = jnp.where(live_mask[:, None, None], received, jnp.zeros_like(received))
            cell_ids = (ab_ids * CD_DEV + cd_ids).astype(jnp.int32)
            grid = jnp.zeros((AB_DEV * CD_DEV, TILE, TILE), received.dtype).at[cell_ids].set(masked)
            weight = grid.reshape(AB_DEV, CD_DEV, TILE, TILE).transpose(1, 2, 0, 3).reshape(CD_DEV * TILE, AB_DEV * TILE)
            start = (rep_idx * CD_DEV * TILE).astype(jnp.int32)
            amp_rep = lax.dynamic_slice_in_dim(amplitudes, start, CD_DEV * TILE, 1)
            return running + jnp.dot(amp_rep, weight, preferred_element_type=jnp.float32)

        return lax.fori_loop(0, N_REP, add_rep, jnp.zeros((OP, AB_DEV * TILE), jnp.float32))

    per_owner = lax.map(owner_block, jnp.arange(N_OWN, dtype=jnp.int32))
    return per_owner.transpose(1, 0, 2).reshape(OP, N_OWN * AB_DEV * TILE)
```

```python
import functools

import jax
import jax.numpy as jnp
from jax import lax
from jax.experimental import pallas as pl
from jax.experimental.pallas import tpu as pltpu
from jax.sharding import PartitionSpec as P

AB_DEV = 16


def _slot_order(ab_ids, live_mask, ab_count):
    n = ab_ids.shape[0]
    key = jnp.where(live_mask, ab_ids, ab_count)
    idx = jnp.arange(n, dtype=jnp.int32)
    earlier = (key[None, :] < key[:, None]) | ((key[None, :] == key[:, None]) & (idx[None, :] < idx[:, None]))
    rank = jnp.sum(earlier.astype(jnp.int32), axis=1)
    order = jnp.sum(jnp.where(rank[None, :] == idx[:, None], idx[None, :], 0), axis=1).astype(jnp.int32)
    bounds = jnp.arange(ab_count + 1, dtype=jnp.int32)
    starts = jnp.sum((key[None, :] < bounds[:, None]).astype(jnp.int32), axis=1).astype(jnp.int32)
    return order, starts


def _ladder_kernel(order_ref, starts_ref, cd_ref, amp_ref, tiles_ref, out_ref):
    j = pl.program_id(0)
    tile = tiles_ref.shape[-1]
    out_ref[...] = jnp.zeros(out_ref.shape, jnp.float32)

    def body(t, carry):
        i = order_ref[t]
        col = pl.multiple_of(cd_ref[i] * tile, tile)
        out_ref[...] += jnp.dot(
            amp_ref[:, pl.ds(col, tile)], tiles_ref[i], preferred_element_type=jnp.float32
        )
        return carry

    lax.fori_loop(starts_ref[j], starts_ref[j + 1], body, 0)


def _ladder_products(amp, tiles, order, starts, cd_ids, ab_count):
    rows, width = amp.shape
    n, tile, _ = tiles.shape
    cost = pl.CostEstimate(
        flops=2 * rows * tile * tile * n,
        transcendentals=0,
        bytes_accessed=amp.size * 2 + tiles.size * 2 + rows * ab_count * tile * 4,
    )
    grid_spec = pltpu.PrefetchScalarGridSpec(
        num_scalar_prefetch=3,
        grid=(ab_count,),
        in_specs=[
            pl.BlockSpec((rows, width), lambda j, *_: (0, 0)),
            pl.BlockSpec((n, tile, tile), lambda j, *_: (0, 0, 0)),
        ],
        out_specs=pl.BlockSpec((rows, tile), lambda j, *_: (0, j)),
    )
    return pl.pallas_call(
        _ladder_kernel,
        grid_spec=grid_spec,
        out_shape=jax.ShapeDtypeStruct((rows, ab_count * tile), jnp.float32),
        cost_estimate=cost,
    )(order, starts, cd_ids, amp, tiles)


def on_device(amplitudes, integrals, ab_list, cd_list, live_count):
    gathered = lax.all_gather(amplitudes, "own", axis=0, tiled=True)
    own_count = lax.axis_size("own")
    rep_count = lax.axis_size("rep")
    peer_count = own_count * rep_count
    slot_count = integrals.shape[0] // peer_count
    received = lax.all_to_all(integrals, ("own", "rep"), split_axis=0, concat_axis=0, tiled=True)
    ab_ids = ab_list.reshape(-1)
    cd_ids = cd_list.reshape(-1)
    live_mask = (
        jnp.arange(slot_count, dtype=jnp.int32)[None, :] < live_count.reshape(peer_count, 1)
    ).reshape(-1)
    order, starts = _slot_order(ab_ids, live_mask, AB_DEV)
    flattened = _ladder_products(gathered, received, order, starts, cd_ids, AB_DEV)
    return lax.psum_scatter(flattened, "rep", scatter_dimension=0, tiled=True)


def solution(mesh):
    return jax.shard_map(
        on_device,
        mesh=mesh,
        in_specs=(
            P("own", "rep"),
            P(("own", "rep"), None, None),
            P(("own", "rep"), None, None),
            P(("own", "rep"), None, None),
            P(("own", "rep"), None),
        ),
        out_specs=P("rep", "own"),
        check_vma=False,
    )
```

```python
import functools

import jax
import jax.numpy as jnp
from jax import lax
from jax.experimental import pallas as pl
from jax.experimental.pallas import tpu as pltpu
from jax.sharding import PartitionSpec as P

AB_DEV = 16
N_CHUNK = 2


def _slot_order(ab_ids, live_mask, ab_count):
    n = ab_ids.shape[0]
    key = jnp.where(live_mask, ab_ids, ab_count)
    idx = jnp.arange(n, dtype=jnp.int32)
    earlier = (key[None, :] < key[:, None]) | ((key[None, :] == key[:, None]) & (idx[None, :] < idx[:, None]))
    rank = jnp.sum(earlier.astype(jnp.int32), axis=1)
    order = jnp.sum(jnp.where(rank[None, :] == idx[:, None], idx[None, :], 0), axis=1).astype(jnp.int32)
    bounds = jnp.arange(ab_count + 1, dtype=jnp.int32)
    starts = jnp.sum((key[None, :] < bounds[:, None]).astype(jnp.int32), axis=1).astype(jnp.int32)
    return order, starts


def _ladder_kernel(order_ref, starts_ref, cd_ref, amp_ref, tiles_ref, out_ref):
    j = pl.program_id(0)
    tile = tiles_ref.shape[-1]
    groups, part, _ = amp_ref.shape
    out_ref[...] = jnp.zeros(out_ref.shape, jnp.float32)

    def body(t, carry):
        i = order_ref[t]
        col = pl.multiple_of(cd_ref[i] * tile, tile)
        lhs = amp_ref[:, :, pl.ds(col, tile)].reshape(groups * part, tile)
        out_ref[...] += jnp.dot(lhs, tiles_ref[i], preferred_element_type=jnp.float32)
        return carry

    lax.fori_loop(starts_ref[j], starts_ref[j + 1], body, 0)


def _ladder_products(amp4, chunk, tiles, order, starts, cd_ids, ab_count):
    groups, _, part, width = amp4.shape
    rows = groups * part
    n, tile, _ = tiles.shape
    cost = pl.CostEstimate(
        flops=2 * rows * tile * tile * n,
        transcendentals=0,
        bytes_accessed=rows * width * 2 + tiles.size * 2 + rows * ab_count * tile * 4,
    )
    grid_spec = pltpu.PrefetchScalarGridSpec(
        num_scalar_prefetch=3,
        grid=(ab_count,),
        in_specs=[
            pl.BlockSpec((groups, None, part, width), lambda j, *_: (0, chunk, 0, 0)),
            pl.BlockSpec((n, tile, tile), lambda j, *_: (0, 0, 0)),
        ],
        out_specs=pl.BlockSpec((rows, tile), lambda j, *_: (0, j)),
    )
    return pl.pallas_call(
        _ladder_kernel,
        grid_spec=grid_spec,
        out_shape=jax.ShapeDtypeStruct((rows, ab_count * tile), jnp.float32),
        cost_estimate=cost,
    )(order, starts, cd_ids, amp4, tiles)


def _halving_scatter(partial, bit_order, rep_index, rep_count):
    levels = rep_count.bit_length() - 1
    width = partial.shape[-1]
    part = partial.shape[0] // rep_count
    x = partial.reshape((2,) * levels + (part, width))
    axis_bits = list(range(levels - 1, -1, -1))
    for bit in bit_order:
        ax = axis_bits.index(bit)
        mine = (rep_index >> bit) & 1
        keep = lax.dynamic_index_in_dim(x, mine, ax, keepdims=False)
        send = lax.dynamic_index_in_dim(x, 1 - mine, ax, keepdims=False)
        pairs = [(i, i ^ (1 << bit)) for i in range(rep_count)]
        x = keep + lax.ppermute(send, "rep", perm=pairs)
        axis_bits.pop(ax)
    return x.reshape(part, width)


def on_device(amplitudes, integrals, ab_list, cd_list, live_count):
    gathered = lax.all_gather(amplitudes, "own", axis=0, tiled=True)
    own_count = lax.axis_size("own")
    rep_count = lax.axis_size("rep")
    peer_count = own_count * rep_count
    slot_count = integrals.shape[0] // peer_count
    received = lax.all_to_all(integrals, ("own", "rep"), split_axis=0, concat_axis=0, tiled=True)
    ab_ids = ab_list.reshape(-1)
    cd_ids = cd_list.reshape(-1)
    live_mask = (
        jnp.arange(slot_count, dtype=jnp.int32)[None, :] < live_count.reshape(peer_count, 1)
    ).reshape(-1)
    order, starts = _slot_order(ab_ids, live_mask, AB_DEV)
    rows, width = gathered.shape
    part = rows // (rep_count * N_CHUNK)
    amp4 = gathered.reshape(rep_count, N_CHUNK, part, width)
    rep_index = lax.axis_index("rep")
    levels = rep_count.bit_length() - 1
    orders = (list(range(levels)), [0] + list(range(levels - 1, 0, -1)))
    pieces = []
    for chunk in range(N_CHUNK):
        partial = _ladder_products(amp4, chunk, received, order, starts, cd_ids, AB_DEV)
        half = partial.shape[1] // 2
        sides = [
            _halving_scatter(partial[:, h * half:(h + 1) * half], orders[h], rep_index, rep_count)
            for h in range(2)
        ]
        pieces.append(jnp.concatenate(sides, axis=1))
    return jnp.concatenate(pieces, axis=0)


def solution(mesh):
    return jax.shard_map(
        on_device,
        mesh=mesh,
        in_specs=(
            P("own", "rep"),
            P(("own", "rep"), None, None),
            P(("own", "rep"), None, None),
            P(("own", "rep"), None, None),
            P(("own", "rep"), None),
        ),
        out_specs=P("rep", "own"),
        check_vma=False,
    )
```

```python
import functools

import jax
import jax.numpy as jnp
from jax import lax
from jax.experimental import pallas as pl
from jax.experimental.pallas import tpu as pltpu
from jax.sharding import PartitionSpec as P

AB_DEV = 16
N_CHUNK = 4


def _slot_order(ab_ids, live_mask, ab_count):
    n = ab_ids.shape[0]
    key = jnp.where(live_mask, ab_ids, ab_count)
    idx = jnp.arange(n, dtype=jnp.int32)
    earlier = (key[None, :] < key[:, None]) | ((key[None, :] == key[:, None]) & (idx[None, :] < idx[:, None]))
    rank = jnp.sum(earlier.astype(jnp.int32), axis=1)
    order = jnp.sum(jnp.where(rank[None, :] == idx[:, None], idx[None, :], 0), axis=1).astype(jnp.int32)
    bounds = jnp.arange(ab_count + 1, dtype=jnp.int32)
    starts = jnp.sum((key[None, :] < bounds[:, None]).astype(jnp.int32), axis=1).astype(jnp.int32)
    return order, starts


def _ladder_kernel(order_ref, starts_ref, cd_ref, amp_ref, tiles_ref, out_ref):
    step = pl.program_id(0)
    tile = tiles_ref.shape[-1]
    groups, part, _ = amp_ref.shape
    per_step = out_ref.shape[1] // tile
    out_ref[...] = jnp.zeros(out_ref.shape, jnp.float32)
    for sub in range(per_step):
        ab = step * per_step + sub

        def body(t, carry, sub=sub):
            i = order_ref[t]
            col = pl.multiple_of(cd_ref[i] * tile, tile)
            lhs = amp_ref[:, :, pl.ds(col, tile)].reshape(groups * part, tile)
            out_ref[:, sub * tile:(sub + 1) * tile] += jnp.dot(
                lhs, tiles_ref[i], preferred_element_type=jnp.float32
            )
            return carry

        lax.fori_loop(starts_ref[ab], starts_ref[ab + 1], body, 0)


def _ladder_products(amp3, tiles, order, starts, cd_ids, ab_count):
    groups, part, width = amp3.shape
    rows = groups * part
    n, tile, _ = tiles.shape
    per_step = 4 if ab_count % 4 == 0 else 1
    cost = pl.CostEstimate(
        flops=2 * rows * tile * tile * n,
        transcendentals=0,
        bytes_accessed=rows * width * 2 + tiles.size * 2 + rows * ab_count * tile * 4,
    )
    grid_spec = pltpu.PrefetchScalarGridSpec(
        num_scalar_prefetch=3,
        grid=(ab_count // per_step,),
        in_specs=[
            pl.BlockSpec((groups, part, width), lambda j, *_: (0, 0, 0)),
            pl.BlockSpec((n, tile, tile), lambda j, *_: (0, 0, 0)),
        ],
        out_specs=pl.BlockSpec((rows, per_step * tile), lambda j, *_: (0, j)),
    )
    return pl.pallas_call(
        _ladder_kernel,
        grid_spec=grid_spec,
        out_shape=jax.ShapeDtypeStruct((rows, ab_count * tile), jnp.float32),
        cost_estimate=cost,
    )(order, starts, cd_ids, amp3, tiles)


def _halving_scatter(partial, bit_order, rep_index, rep_count):
    levels = rep_count.bit_length() - 1
    width = partial.shape[-1]
    part = partial.shape[0] // rep_count
    x = partial.reshape((2,) * levels + (part, width))
    axis_bits = list(range(levels - 1, -1, -1))
    for bit in bit_order:
        ax = axis_bits.index(bit)
        mine = (rep_index >> bit) & 1
        keep = lax.dynamic_index_in_dim(x, mine, ax, keepdims=False)
        send = lax.dynamic_index_in_dim(x, 1 - mine, ax, keepdims=False)
        pairs = [(i, i ^ (1 << bit)) for i in range(rep_count)]
        x = keep + lax.ppermute(send, "rep", perm=pairs)
        axis_bits.pop(ax)
    return x.reshape(part, width)


def on_device(amplitudes, integrals, ab_list, cd_list, live_count):
    own_count = lax.axis_size("own")
    rep_count = lax.axis_size("rep")
    peer_count = own_count * rep_count
    slot_count = integrals.shape[0] // peer_count
    received = lax.all_to_all(integrals, ("own", "rep"), split_axis=0, concat_axis=0, tiled=True)
    amplitudes, received = lax.optimization_barrier((amplitudes, received))
    ab_ids = ab_list.reshape(-1)
    cd_ids = cd_list.reshape(-1)
    live_mask = (
        jnp.arange(slot_count, dtype=jnp.int32)[None, :] < live_count.reshape(peer_count, 1)
    ).reshape(-1)
    order, starts = _slot_order(ab_ids, live_mask, AB_DEV)
    local_rows, width = amplitudes.shape
    subs = rep_count // own_count
    part = local_rows // (subs * N_CHUNK)
    local4 = amplitudes.reshape(subs, N_CHUNK, part, width)
    rep_index = lax.axis_index("rep")
    levels = rep_count.bit_length() - 1
    orders = (list(range(levels)), [0] + list(range(levels - 1, 0, -1)))
    pieces = []
    for chunk in range(N_CHUNK):
        amp3 = lax.all_gather(local4[:, chunk], "own", axis=0, tiled=True)
        if pieces:
            amp3, pieces[-1] = lax.optimization_barrier((amp3, pieces[-1]))
        partial = _ladder_products(amp3, received, order, starts, cd_ids, AB_DEV)
        half = partial.shape[1] // 2
        sides = [
            _halving_scatter(partial[:, h * half:(h + 1) * half], orders[h], rep_index, rep_count)
            for h in range(2)
        ]
        pieces.append(jnp.concatenate(sides, axis=1))
    return jnp.concatenate(pieces, axis=0)


def solution(mesh):
    return jax.shard_map(
        on_device,
        mesh=mesh,
        in_specs=(
            P("own", "rep"),
            P(("own", "rep"), None, None),
            P(("own", "rep"), None, None),
            P(("own", "rep"), None, None),
            P(("own", "rep"), None),
        ),
        out_specs=P("rep", "own"),
        check_vma=False,
    )
```

```python
import functools

import jax
import jax.numpy as jnp
from jax import lax
from jax.experimental import pallas as pl
from jax.experimental.pallas import tpu as pltpu
from jax.sharding import PartitionSpec as P

AB_DEV = 16
N_CHUNK = 4


def _slot_order(ab_ids, live_mask, ab_count):
    n = ab_ids.shape[0]
    key = jnp.where(live_mask, ab_ids, ab_count)
    idx = jnp.arange(n, dtype=jnp.int32)
    earlier = (key[None, :] < key[:, None]) | ((key[None, :] == key[:, None]) & (idx[None, :] < idx[:, None]))
    rank = jnp.sum(earlier.astype(jnp.int32), axis=1)
    order = jnp.sum(jnp.where(rank[None, :] == idx[:, None], idx[None, :], 0), axis=1).astype(jnp.int32)
    bounds = jnp.arange(ab_count + 1, dtype=jnp.int32)
    starts = jnp.sum((key[None, :] < bounds[:, None]).astype(jnp.int32), axis=1).astype(jnp.int32)
    return order, starts


def _ladder_kernel(order_ref, starts_ref, ab_ref, cd_ref, amp_ref, tiles_ref, out_ref, weight_ref):
    step = pl.program_id(0)
    tile = tiles_ref.shape[-1]
    groups, part, width = amp_ref.shape
    per_step = out_ref.shape[1] // tile
    weight_ref[...] = jnp.zeros(weight_ref.shape, weight_ref.dtype)
    first = step * per_step

    def place(t, carry):
        i = order_ref[t]
        row = pl.multiple_of(cd_ref[i] * tile, tile)
        col = pl.multiple_of((ab_ref[i] - first) * tile, tile)
        weight_ref[pl.ds(row, tile), pl.ds(col, tile)] = tiles_ref[i]
        return carry

    lax.fori_loop(starts_ref[first], starts_ref[first + per_step], place, 0)
    lhs = amp_ref[...].reshape(groups * part, width)
    out_ref[...] = jnp.dot(lhs, weight_ref[...], preferred_element_type=jnp.float32)


def _ladder_products(amp3, tiles, order, starts, ab_ids, cd_ids, ab_count):
    groups, part, width = amp3.shape
    rows = groups * part
    n, tile, _ = tiles.shape
    per_step = 2 if ab_count % 2 == 0 else 1
    cost = pl.CostEstimate(
        flops=2 * rows * width * ab_count * tile,
        transcendentals=0,
        bytes_accessed=rows * width * 2 + tiles.size * 2 + rows * ab_count * tile * 4,
    )
    grid_spec = pltpu.PrefetchScalarGridSpec(
        num_scalar_prefetch=4,
        grid=(ab_count // per_step,),
        in_specs=[
            pl.BlockSpec((groups, part, width), lambda j, *_: (0, 0, 0)),
            pl.BlockSpec((n, tile, tile), lambda j, *_: (0, 0, 0)),
        ],
        out_specs=pl.BlockSpec((rows, per_step * tile), lambda j, *_: (0, j)),
        scratch_shapes=[pltpu.VMEM((width, per_step * tile), tiles.dtype)],
    )
    return pl.pallas_call(
        _ladder_kernel,
        grid_spec=grid_spec,
        out_shape=jax.ShapeDtypeStruct((rows, ab_count * tile), jnp.float32),
        cost_estimate=cost,
    )(order, starts, ab_ids, cd_ids, amp3, tiles)


class _Halving:
    def __init__(self, partial, bit_order, rep_count):
        self.levels = rep_count.bit_length() - 1
        self.part = partial.shape[0] // rep_count
        self.width = partial.shape[-1]
        self.x = partial.reshape((2,) * self.levels + (self.part, self.width))
        self.axis_bits = list(range(self.levels - 1, -1, -1))
        self.todo = list(bit_order)
        self.rep_count = rep_count

    def advance(self, rep_index):
        if not self.todo:
            return
        bit = self.todo.pop(0)
        ax = self.axis_bits.index(bit)
        mine = (rep_index >> bit) & 1
        keep = lax.dynamic_index_in_dim(self.x, mine, ax, keepdims=False)
        send = lax.dynamic_index_in_dim(self.x, 1 - mine, ax, keepdims=False)
        pairs = [(i, i ^ (1 << bit)) for i in range(self.rep_count)]
        self.x = keep + lax.ppermute(send, "rep", perm=pairs)
        self.axis_bits.pop(ax)

    def result(self):
        return self.x.reshape(self.part, self.width)


def on_device(amplitudes, integrals, ab_list, cd_list, live_count):
    own_count = lax.axis_size("own")
    rep_count = lax.axis_size("rep")
    peer_count = own_count * rep_count
    slot_count = integrals.shape[0] // peer_count
    received = lax.all_to_all(integrals, ("own", "rep"), split_axis=0, concat_axis=0, tiled=True)
    ab_ids = ab_list.reshape(-1)
    cd_ids = cd_list.reshape(-1)
    live_mask = (
        jnp.arange(slot_count, dtype=jnp.int32)[None, :] < live_count.reshape(peer_count, 1)
    ).reshape(-1)
    order, starts = _slot_order(ab_ids, live_mask, AB_DEV)
    local_rows, width = amplitudes.shape
    subs = rep_count // own_count
    part = local_rows // (subs * N_CHUNK)
    local4 = amplitudes.reshape(subs, N_CHUNK, part, width)
    rep_index = lax.axis_index("rep")
    levels = rep_count.bit_length() - 1
    orders = (list(range(levels)), [0] + list(range(levels - 1, 0, -1)))
    gathered = [lax.all_gather(local4[:, c], "own", axis=0, tiled=True) for c in range(N_CHUNK)]
    flows = []
    for chunk in range(N_CHUNK):
        for flow in flows:
            flow.advance(rep_index)
        if flows:
            amp3, held = lax.optimization_barrier((gathered[chunk], [f.x for f in flows]))
            for flow, x in zip(flows, held):
                flow.x = x
        else:
            amp3 = gathered[chunk]
        partial = _ladder_products(amp3, received, order, starts, ab_ids, cd_ids, AB_DEV)
        half = partial.shape[1] // 2
        flows.extend(
            _Halving(partial[:, h * half:(h + 1) * half], orders[h], rep_count) for h in range(2)
        )
    while any(flow.todo for flow in flows):
        for flow in flows:
            flow.advance(rep_index)
    pieces = [
        jnp.concatenate([flows[2 * c].result(), flows[2 * c + 1].result()], axis=1)
        for c in range(N_CHUNK)
    ]
    return jnp.concatenate(pieces, axis=0)


def solution(mesh):
    return jax.shard_map(
        on_device,
        mesh=mesh,
        in_specs=(
            P("own", "rep"),
            P(("own", "rep"), None, None),
            P(("own", "rep"), None, None),
            P(("own", "rep"), None, None),
            P(("own", "rep"), None),
        ),
        out_specs=P("rep", "own"),
        check_vma=False,
    )
```

```python
import functools

import jax
import jax.numpy as jnp
from jax import lax
from jax.experimental import pallas as pl
from jax.experimental.pallas import tpu as pltpu
from jax.sharding import PartitionSpec as P

AB_DEV = 16
CHUNKS = (2, 1, 1)


def _slot_order(ab_ids, live_mask, ab_count):
    n = ab_ids.shape[0]
    key = jnp.where(live_mask, ab_ids, ab_count)
    idx = jnp.arange(n, dtype=jnp.int32)
    earlier = (key[None, :] < key[:, None]) | ((key[None, :] == key[:, None]) & (idx[None, :] < idx[:, None]))
    rank = jnp.sum(earlier.astype(jnp.int32), axis=1)
    order = jnp.sum(jnp.where(rank[None, :] == idx[:, None], idx[None, :], 0), axis=1).astype(jnp.int32)
    bounds = jnp.arange(ab_count + 1, dtype=jnp.int32)
    starts = jnp.sum((key[None, :] < bounds[:, None]).astype(jnp.int32), axis=1).astype(jnp.int32)
    return order, starts


def _weight_kernel(order_ref, starts_ref, cd_ref, tiles_ref, out_ref):
    ab = pl.program_id(0)
    tile = tiles_ref.shape[-1]
    out_ref[...] = jnp.zeros(out_ref.shape, out_ref.dtype)

    def place(t, carry):
        i = order_ref[t]
        row = pl.multiple_of(cd_ref[i] * tile, tile)
        out_ref[pl.ds(row, tile), :] = tiles_ref[i]
        return carry

    lax.fori_loop(starts_ref[ab], starts_ref[ab + 1], place, 0)


def _dense_weight(tiles, order, starts, cd_ids, cd_count, ab_count):
    n, tile, _ = tiles.shape
    width = cd_count * tile
    grid_spec = pltpu.PrefetchScalarGridSpec(
        num_scalar_prefetch=3,
        grid=(ab_count,),
        in_specs=[pl.BlockSpec((n, tile, tile), lambda j, *_: (0, 0, 0))],
        out_specs=pl.BlockSpec((width, tile), lambda j, *_: (0, j)),
    )
    return pl.pallas_call(
        _weight_kernel,
        grid_spec=grid_spec,
        out_shape=jax.ShapeDtypeStruct((width, ab_count * tile), tiles.dtype),
        cost_estimate=pl.CostEstimate(
            flops=0, transcendentals=0, bytes_accessed=tiles.size * 2 + width * ab_count * tile * 2
        ),
    )(order, starts, cd_ids, tiles)


class _Halving:
    def __init__(self, partial, bit_order, rep_count):
        self.levels = rep_count.bit_length() - 1
        self.part = partial.shape[0] // rep_count
        self.width = partial.shape[-1]
        self.x = partial.reshape((2,) * self.levels + (self.part, self.width))
        self.axis_bits = list(range(self.levels - 1, -1, -1))
        self.todo = list(bit_order)
        self.rep_count = rep_count

    def advance(self, rep_index):
        if not self.todo:
            return
        bit = self.todo.pop(0)
        ax = self.axis_bits.index(bit)
        mine = (rep_index >> bit) & 1
        keep = lax.dynamic_index_in_dim(self.x, mine, ax, keepdims=False)
        send = lax.dynamic_index_in_dim(self.x, 1 - mine, ax, keepdims=False)
        pairs = [(i, i ^ (1 << bit)) for i in range(self.rep_count)]
        self.x = keep + lax.ppermute(send, "rep", perm=pairs)
        self.axis_bits.pop(ax)

    def result(self):
        return self.x.reshape(self.part, self.width)


def on_device(amplitudes, integrals, ab_list, cd_list, live_count):
    own_count = lax.axis_size("own")
    rep_count = lax.axis_size("rep")
    peer_count = own_count * rep_count
    slot_count = integrals.shape[0] // peer_count
    received = lax.all_to_all(integrals, ("own", "rep"), split_axis=0, concat_axis=0, tiled=True)
    ab_ids = ab_list.reshape(-1)
    cd_ids = cd_list.reshape(-1)
    live_mask = (
        jnp.arange(slot_count, dtype=jnp.int32)[None, :] < live_count.reshape(peer_count, 1)
    ).reshape(-1)
    order, starts = _slot_order(ab_ids, live_mask, AB_DEV)
    local_rows, width = amplitudes.shape
    tile = integrals.shape[-1]
    weight = _dense_weight(received, order, starts, cd_ids, width // tile, AB_DEV)
    subs = rep_count // own_count
    units = sum(CHUNKS)
    part = local_rows // (subs * units)
    local4 = amplitudes.reshape(subs, units, part, width)
    rep_index = lax.axis_index("rep")
    levels = rep_count.bit_length() - 1
    orders = (list(range(levels)), [0] + list(range(levels - 1, 0, -1)))
    bounds = [sum(CHUNKS[:c]) for c in range(len(CHUNKS) + 1)]
    gathered = [
        lax.all_gather(local4[:, bounds[c]:bounds[c + 1]], "own", axis=0, tiled=True)
        for c in range(len(CHUNKS))
    ]
    half = weight.shape[1] // 2
    flows = []
    for chunk in range(len(CHUNKS)):
        for flow in flows:
            flow.advance(rep_index)
        if flows:
            amp4, held = lax.optimization_barrier((gathered[chunk], [f.x for f in flows]))
            for flow, x in zip(flows, held):
                flow.x = x
        else:
            amp4 = gathered[chunk]
        lhs = amp4.reshape(-1, width)
        for h in range(2):
            partial = jnp.dot(lhs, weight[:, h * half:(h + 1) * half], preferred_element_type=jnp.float32)
            flows.append(_Halving(partial, orders[h], rep_count))
    while any(flow.todo for flow in flows):
        for flow in flows:
            flow.advance(rep_index)
    pieces = []
    for chunk in range(len(CHUNKS)):
        size = CHUNKS[chunk]
        sides = [flows[2 * chunk + h].result().reshape(size, part, half) for h in range(2)]
        pieces.append(jnp.concatenate(sides, axis=2))
    return jnp.concatenate(pieces, axis=0).reshape(units * part, 2 * half)


def solution(mesh):
    return jax.shard_map(
        on_device,
        mesh=mesh,
        in_specs=(
            P("own", "rep"),
            P(("own", "rep"), None, None),
            P(("own", "rep"), None, None),
            P(("own", "rep"), None, None),
            P(("own", "rep"), None),
        ),
        out_specs=P("rep", "own"),
        check_vma=False,
    )
```

```python
import functools

import jax
import jax.numpy as jnp
from jax import lax
from jax.experimental import pallas as pl
from jax.experimental.pallas import tpu as pltpu
from jax.sharding import PartitionSpec as P

AB_DEV = 16
CHUNKS = (4, 2, 1, 1)


def _slot_order(ab_ids, live_mask, ab_count):
    n = ab_ids.shape[0]
    key = jnp.where(live_mask, ab_ids, ab_count)
    idx = jnp.arange(n, dtype=jnp.int32)
    earlier = (key[None, :] < key[:, None]) | ((key[None, :] == key[:, None]) & (idx[None, :] < idx[:, None]))
    rank = jnp.sum(earlier.astype(jnp.int32), axis=1)
    order = jnp.sum(jnp.where(rank[None, :] == idx[:, None], idx[None, :], 0), axis=1).astype(jnp.int32)
    bounds = jnp.arange(ab_count + 1, dtype=jnp.int32)
    starts = jnp.sum((key[None, :] < bounds[:, None]).astype(jnp.int32), axis=1).astype(jnp.int32)
    return order, starts


def _weight_kernel(order_ref, starts_ref, cd_ref, tiles_ref, out_ref):
    ab = pl.program_id(0)
    tile = tiles_ref.shape[-1]
    out_ref[...] = jnp.zeros(out_ref.shape, out_ref.dtype)

    def place(t, carry):
        i = order_ref[t]
        row = pl.multiple_of(cd_ref[i] * tile, tile)
        out_ref[pl.ds(row, tile), :] = tiles_ref[i]
        return carry

    lax.fori_loop(starts_ref[ab], starts_ref[ab + 1], place, 0)


def _dense_weight(tiles, order, starts, cd_ids, cd_count, ab_count):
    n, tile, _ = tiles.shape
    width = cd_count * tile
    grid_spec = pltpu.PrefetchScalarGridSpec(
        num_scalar_prefetch=3,
        grid=(ab_count,),
        in_specs=[pl.BlockSpec((n, tile, tile), lambda j, *_: (0, 0, 0))],
        out_specs=pl.BlockSpec((width, tile), lambda j, *_: (0, j)),
    )
    return pl.pallas_call(
        _weight_kernel,
        grid_spec=grid_spec,
        out_shape=jax.ShapeDtypeStruct((width, ab_count * tile), tiles.dtype),
        cost_estimate=pl.CostEstimate(
            flops=0, transcendentals=0, bytes_accessed=tiles.size * 2 + width * ab_count * tile * 2
        ),
    )(order, starts, cd_ids, tiles)


class _Halving:
    def __init__(self, partial, bit_order, rep_count):
        self.levels = rep_count.bit_length() - 1
        self.part = partial.shape[0] // rep_count
        self.width = partial.shape[-1]
        self.x = partial.reshape((2,) * self.levels + (self.part, self.width))
        self.axis_bits = list(range(self.levels - 1, -1, -1))
        self.todo = list(bit_order)
        self.rep_count = rep_count

    def advance(self, rep_index):
        if not self.todo:
            return
        bit = self.todo.pop(0)
        ax = self.axis_bits.index(bit)
        mine = (rep_index >> bit) & 1
        keep = lax.dynamic_index_in_dim(self.x, mine, ax, keepdims=False)
        send = lax.dynamic_index_in_dim(self.x, 1 - mine, ax, keepdims=False)
        pairs = [(i, i ^ (1 << bit)) for i in range(self.rep_count)]
        self.x = keep + lax.ppermute(send, "rep", perm=pairs)
        self.axis_bits.pop(ax)

    def result(self):
        return self.x.reshape(self.part, self.width)


def on_device(amplitudes, integrals, ab_list, cd_list, live_count):
    own_count = lax.axis_size("own")
    rep_count = lax.axis_size("rep")
    peer_count = own_count * rep_count
    slot_count = integrals.shape[0] // peer_count
    received = lax.all_to_all(integrals, ("own", "rep"), split_axis=0, concat_axis=0, tiled=True)
    ab_ids = ab_list.reshape(-1)
    cd_ids = cd_list.reshape(-1)
    live_mask = (
        jnp.arange(slot_count, dtype=jnp.int32)[None, :] < live_count.reshape(peer_count, 1)
    ).reshape(-1)
    order, starts = _slot_order(ab_ids, live_mask, AB_DEV)
    local_rows, width = amplitudes.shape
    tile = integrals.shape[-1]
    weight = _dense_weight(received, order, starts, cd_ids, width // tile, AB_DEV)
    subs = rep_count // own_count
    units = sum(CHUNKS)
    part = local_rows // (subs * units)
    local4 = amplitudes.reshape(subs, units, part, width)
    rep_index = lax.axis_index("rep")
    levels = rep_count.bit_length() - 1
    orders = (list(range(levels)), [0] + list(range(levels - 1, 0, -1)))
    bounds = [sum(CHUNKS[:c]) for c in range(len(CHUNKS) + 1)]
    gathered = [
        lax.all_gather(local4[:, bounds[c]:bounds[c + 1]], "own", axis=0, tiled=True)
        for c in range(len(CHUNKS))
    ]
    half = weight.shape[1] // 2
    flows = []
    for chunk in range(len(CHUNKS)):
        for flow in flows:
            flow.advance(rep_index)
        if flows:
            amp4, held = lax.optimization_barrier((gathered[chunk], [f.x for f in flows]))
            for flow, x in zip(flows, held):
                flow.x = x
        else:
            amp4 = gathered[chunk]
        lhs = amp4.reshape(-1, width)
        for h in range(2):
            partial = jnp.dot(lhs, weight[:, h * half:(h + 1) * half], preferred_element_type=jnp.float32)
            flows.append(_Halving(partial, orders[h], rep_count))
    while any(flow.todo for flow in flows):
        for flow in flows:
            flow.advance(rep_index)
    pieces = []
    for chunk in range(len(CHUNKS)):
        size = CHUNKS[chunk]
        sides = [flows[2 * chunk + h].result().reshape(size, part, half) for h in range(2)]
        pieces.append(jnp.concatenate(sides, axis=2))
    return jnp.concatenate(pieces, axis=0).reshape(units * part, 2 * half)


def solution(mesh):
    return jax.shard_map(
        on_device,
        mesh=mesh,
        in_specs=(
            P("own", "rep"),
            P(("own", "rep"), None, None),
            P(("own", "rep"), None, None),
            P(("own", "rep"), None, None),
            P(("own", "rep"), None),
        ),
        out_specs=P("rep", "own"),
        check_vma=False,
    )
```

```python
import functools

import jax
import jax.numpy as jnp
from jax import lax
from jax.experimental import pallas as pl
from jax.experimental.pallas import tpu as pltpu
from jax.sharding import PartitionSpec as P

AB_DEV = 16
CHUNKS = (2, 1, 1)


def _slot_order(ab_ids, live_mask, ab_count):
    n = ab_ids.shape[0]
    key = jnp.where(live_mask, ab_ids, ab_count)
    idx = jnp.arange(n, dtype=jnp.int32)
    earlier = (key[None, :] < key[:, None]) | ((key[None, :] == key[:, None]) & (idx[None, :] < idx[:, None]))
    rank = jnp.sum(earlier.astype(jnp.int32), axis=1)
    order = jnp.sum(jnp.where(rank[None, :] == idx[:, None], idx[None, :], 0), axis=1).astype(jnp.int32)
    bounds = jnp.arange(ab_count + 1, dtype=jnp.int32)
    starts = jnp.sum((key[None, :] < bounds[:, None]).astype(jnp.int32), axis=1).astype(jnp.int32)
    return order, starts


def _weight_kernel(order_ref, starts_ref, cd_ref, tiles_ref, out_ref):
    ab = pl.program_id(0)
    tile = tiles_ref.shape[-1]
    out_ref[...] = jnp.zeros(out_ref.shape, out_ref.dtype)

    def place(t, carry):
        i = order_ref[t]
        row = pl.multiple_of(cd_ref[i] * tile, tile)
        out_ref[pl.ds(row, tile), :] = tiles_ref[i]
        return carry

    lax.fori_loop(starts_ref[ab], starts_ref[ab + 1], place, 0)


def _dense_weight(tiles, order, starts, cd_ids, cd_count, ab_count):
    n, tile, _ = tiles.shape
    width = cd_count * tile
    grid_spec = pltpu.PrefetchScalarGridSpec(
        num_scalar_prefetch=3,
        grid=(ab_count,),
        in_specs=[pl.BlockSpec((n, tile, tile), lambda j, *_: (0, 0, 0))],
        out_specs=pl.BlockSpec((width, tile), lambda j, *_: (0, j)),
    )
    return pl.pallas_call(
        _weight_kernel,
        grid_spec=grid_spec,
        out_shape=jax.ShapeDtypeStruct((width, ab_count * tile), tiles.dtype),
        cost_estimate=pl.CostEstimate(
            flops=0, transcendentals=0, bytes_accessed=tiles.size * 2 + width * ab_count * tile * 2
        ),
    )(order, starts, cd_ids, tiles)


class _Halving:
    def __init__(self, partial, bit_order, rep_count):
        self.levels = rep_count.bit_length() - 1
        self.part = partial.shape[0] // rep_count
        self.width = partial.shape[-1]
        self.x = partial.reshape((2,) * self.levels + (self.part, self.width))
        self.axis_bits = list(range(self.levels - 1, -1, -1))
        self.todo = list(bit_order)
        self.rep_count = rep_count

    def advance(self, rep_index):
        if not self.todo:
            return
        bit = self.todo.pop(0)
        ax = self.axis_bits.index(bit)
        mine = (rep_index >> bit) & 1
        keep = lax.dynamic_index_in_dim(self.x, mine, ax, keepdims=False)
        send = lax.dynamic_index_in_dim(self.x, 1 - mine, ax, keepdims=False)
        pairs = [(i, i ^ (1 << bit)) for i in range(self.rep_count)]
        self.x = keep + lax.ppermute(send, "rep", perm=pairs)
        self.axis_bits.pop(ax)

    def result(self):
        return self.x.reshape(self.part, self.width)


def _line_gather(block, own_count):
    me = lax.axis_index("own")
    up = [block]
    down = [block]
    for k in range(1, own_count):
        up.append(lax.ppermute(up[-1], "own", perm=[(i, i + 1) for i in range(k - 1, own_count - 1)]))
        down.append(lax.ppermute(down[-1], "own", perm=[(i + 1, i) for i in range(own_count - k)]))
    out = jnp.zeros((own_count,) + block.shape, block.dtype)
    zero = (0,) * block.ndim
    for k in range(own_count - 1, 0, -1):
        out = lax.dynamic_update_slice(out, up[k][None], (me - k,) + zero)
    for k in range(own_count - 1, 0, -1):
        out = lax.dynamic_update_slice(out, down[k][None], (me + k,) + zero)
    out = lax.dynamic_update_slice(out, block[None], (me,) + zero)
    return out.reshape((own_count * block.shape[0],) + block.shape[1:])


def on_device(amplitudes, integrals, ab_list, cd_list, live_count):
    own_count = lax.axis_size("own")
    rep_count = lax.axis_size("rep")
    peer_count = own_count * rep_count
    slot_count = integrals.shape[0] // peer_count
    received = lax.all_to_all(integrals, ("own", "rep"), split_axis=0, concat_axis=0, tiled=True)
    ab_ids = ab_list.reshape(-1)
    cd_ids = cd_list.reshape(-1)
    live_mask = (
        jnp.arange(slot_count, dtype=jnp.int32)[None, :] < live_count.reshape(peer_count, 1)
    ).reshape(-1)
    order, starts = _slot_order(ab_ids, live_mask, AB_DEV)
    local_rows, width = amplitudes.shape
    tile = integrals.shape[-1]
    weight = _dense_weight(received, order, starts, cd_ids, width // tile, AB_DEV)
    subs = rep_count // own_count
    units = sum(CHUNKS)
    part = local_rows // (subs * units)
    local4 = amplitudes.reshape(subs, units, part, width)
    rep_index = lax.axis_index("rep")
    levels = rep_count.bit_length() - 1
    orders = (list(range(levels)), [0] + list(range(levels - 1, 0, -1)))
    bounds = [sum(CHUNKS[:c]) for c in range(len(CHUNKS) + 1)]
    gathered = [
        lax.all_gather(local4[:, bounds[c]:bounds[c + 1]], "own", axis=0, tiled=True)
        if c == 0
        else _line_gather(local4[:, bounds[c]:bounds[c + 1]], own_count)
        for c in range(len(CHUNKS))
    ]
    half = weight.shape[1] // 2
    flows = []
    for chunk in range(len(CHUNKS)):
        for flow in flows:
            flow.advance(rep_index)
        if flows:
            amp4, held = lax.optimization_barrier((gathered[chunk], [f.x for f in flows]))
            for flow, x in zip(flows, held):
                flow.x = x
        else:
            amp4 = gathered[chunk]
        lhs = amp4.reshape(-1, width)
        for h in range(2):
            partial = jnp.dot(lhs, weight[:, h * half:(h + 1) * half], preferred_element_type=jnp.float32)
            flows.append(_Halving(partial, orders[h], rep_count))
    while any(flow.todo for flow in flows):
        for flow in flows:
            flow.advance(rep_index)
    pieces = []
    for chunk in range(len(CHUNKS)):
        size = CHUNKS[chunk]
        sides = [flows[2 * chunk + h].result().reshape(size, part, half) for h in range(2)]
        pieces.append(jnp.concatenate(sides, axis=2))
    return jnp.concatenate(pieces, axis=0).reshape(units * part, 2 * half)


def solution(mesh):
    return jax.shard_map(
        on_device,
        mesh=mesh,
        in_specs=(
            P("own", "rep"),
            P(("own", "rep"), None, None),
            P(("own", "rep"), None, None),
            P(("own", "rep"), None, None),
            P(("own", "rep"), None),
        ),
        out_specs=P("rep", "own"),
        check_vma=False,
    )
```

```python
import functools

import jax
import jax.numpy as jnp
from jax import lax
from jax.experimental import pallas as pl
from jax.experimental.pallas import tpu as pltpu
from jax.sharding import PartitionSpec as P

AB_DEV = 16
CHUNKS = (3, 1)


def _slot_order(ab_ids, live_mask, ab_count):
    n = ab_ids.shape[0]
    key = jnp.where(live_mask, ab_ids, ab_count)
    idx = jnp.arange(n, dtype=jnp.int32)
    earlier = (key[None, :] < key[:, None]) | ((key[None, :] == key[:, None]) & (idx[None, :] < idx[:, None]))
    rank = jnp.sum(earlier.astype(jnp.int32), axis=1)
    order = jnp.sum(jnp.where(rank[None, :] == idx[:, None], idx[None, :], 0), axis=1).astype(jnp.int32)
    bounds = jnp.arange(ab_count + 1, dtype=jnp.int32)
    starts = jnp.sum((key[None, :] < bounds[:, None]).astype(jnp.int32), axis=1).astype(jnp.int32)
    return order, starts


def _weight_kernel(order_ref, starts_ref, cd_ref, tiles_ref, out_ref):
    ab = pl.program_id(0)
    tile = tiles_ref.shape[-1]
    out_ref[...] = jnp.zeros(out_ref.shape, out_ref.dtype)

    def place(t, carry):
        i = order_ref[t]
        row = pl.multiple_of(cd_ref[i] * tile, tile)
        out_ref[pl.ds(row, tile), :] = tiles_ref[i]
        return carry

    lax.fori_loop(starts_ref[ab], starts_ref[ab + 1], place, 0)


def _dense_weight(tiles, order, starts, cd_ids, cd_count, ab_count):
    n, tile, _ = tiles.shape
    width = cd_count * tile
    grid_spec = pltpu.PrefetchScalarGridSpec(
        num_scalar_prefetch=3,
        grid=(ab_count,),
        in_specs=[pl.BlockSpec((n, tile, tile), lambda j, *_: (0, 0, 0))],
        out_specs=pl.BlockSpec((width, tile), lambda j, *_: (0, j)),
    )
    return pl.pallas_call(
        _weight_kernel,
        grid_spec=grid_spec,
        out_shape=jax.ShapeDtypeStruct((width, ab_count * tile), tiles.dtype),
        cost_estimate=pl.CostEstimate(
            flops=0, transcendentals=0, bytes_accessed=tiles.size * 2 + width * ab_count * tile * 2
        ),
    )(order, starts, cd_ids, tiles)


class _Halving:
    def __init__(self, partial, bit_order, rep_count):
        self.levels = rep_count.bit_length() - 1
        self.part = partial.shape[0] // rep_count
        self.width = partial.shape[-1]
        self.x = partial.reshape((2,) * self.levels + (self.part, self.width))
        self.axis_bits = list(range(self.levels - 1, -1, -1))
        self.todo = list(bit_order)
        self.rep_count = rep_count

    def advance(self, rep_index):
        if not self.todo:
            return
        bit = self.todo.pop(0)
        ax = self.axis_bits.index(bit)
        mine = (rep_index >> bit) & 1
        keep = lax.dynamic_index_in_dim(self.x, mine, ax, keepdims=False)
        send = lax.dynamic_index_in_dim(self.x, 1 - mine, ax, keepdims=False)
        pairs = [(i, i ^ (1 << bit)) for i in range(self.rep_count)]
        self.x = keep + lax.ppermute(send, "rep", perm=pairs)
        self.axis_bits.pop(ax)

    def result(self):
        return self.x.reshape(self.part, self.width)


def on_device(amplitudes, integrals, ab_list, cd_list, live_count):
    own_count = lax.axis_size("own")
    rep_count = lax.axis_size("rep")
    peer_count = own_count * rep_count
    slot_count = integrals.shape[0] // peer_count
    received = lax.all_to_all(integrals, ("own", "rep"), split_axis=0, concat_axis=0, tiled=True)
    ab_ids = ab_list.reshape(-1)
    cd_ids = cd_list.reshape(-1)
    live_mask = (
        jnp.arange(slot_count, dtype=jnp.int32)[None, :] < live_count.reshape(peer_count, 1)
    ).reshape(-1)
    order, starts = _slot_order(ab_ids, live_mask, AB_DEV)
    local_rows, width = amplitudes.shape
    tile = integrals.shape[-1]
    weight = _dense_weight(received, order, starts, cd_ids, width // tile, AB_DEV)
    subs = rep_count // own_count
    units = sum(CHUNKS)
    part = local_rows // (subs * units)
    local4 = amplitudes.reshape(subs, units, part, width)
    rep_index = lax.axis_index("rep")
    levels = rep_count.bit_length() - 1
    orders = (list(range(levels)), [0] + list(range(levels - 1, 0, -1)))
    bounds = [sum(CHUNKS[:c]) for c in range(len(CHUNKS) + 1)]
    gathered = [
        lax.all_gather(local4[:, bounds[c]:bounds[c + 1]], "own", axis=0, tiled=True)
        for c in range(len(CHUNKS))
    ]
    half = weight.shape[1] // 2
    flows = []
    for chunk in range(len(CHUNKS)):
        for flow in flows:
            flow.advance(rep_index)
        if flows:
            amp4, held = lax.optimization_barrier((gathered[chunk], [f.x for f in flows]))
            for flow, x in zip(flows, held):
                flow.x = x
        else:
            amp4 = gathered[chunk]
        lhs = amp4.reshape(-1, width)
        for h in range(2):
            partial = jnp.dot(lhs, weight[:, h * half:(h + 1) * half], preferred_element_type=jnp.float32)
            flows.append(_Halving(partial, orders[h], rep_count))
    while any(flow.todo for flow in flows):
        for flow in flows:
            flow.advance(rep_index)
    pieces = []
    for chunk in range(len(CHUNKS)):
        size = CHUNKS[chunk]
        sides = [flows[2 * chunk + h].result().reshape(size, part, half) for h in range(2)]
        pieces.append(jnp.concatenate(sides, axis=2))
    return jnp.concatenate(pieces, axis=0).reshape(units * part, 2 * half)


def solution(mesh):
    return jax.shard_map(
        on_device,
        mesh=mesh,
        in_specs=(
            P("own", "rep"),
            P(("own", "rep"), None, None),
            P(("own", "rep"), None, None),
            P(("own", "rep"), None, None),
            P(("own", "rep"), None),
        ),
        out_specs=P("rep", "own"),
        check_vma=False,
    )
```

```python
import functools

import jax
import jax.numpy as jnp
from jax import lax
from jax.experimental import pallas as pl
from jax.experimental.pallas import tpu as pltpu
from jax.sharding import PartitionSpec as P

AB_DEV = 16
CHUNKS = (2, 1, 1)


def _slot_order(ab_ids, live_mask, ab_count):
    n = ab_ids.shape[0]
    key = jnp.where(live_mask, ab_ids, ab_count)
    idx = jnp.arange(n, dtype=jnp.int32)
    earlier = (key[None, :] < key[:, None]) | ((key[None, :] == key[:, None]) & (idx[None, :] < idx[:, None]))
    rank = jnp.sum(earlier.astype(jnp.int32), axis=1)
    order = jnp.sum(jnp.where(rank[None, :] == idx[:, None], idx[None, :], 0), axis=1).astype(jnp.int32)
    bounds = jnp.arange(ab_count + 1, dtype=jnp.int32)
    starts = jnp.sum((key[None, :] < bounds[:, None]).astype(jnp.int32), axis=1).astype(jnp.int32)
    return order, starts


def _weight_kernel(order_ref, starts_ref, cd_ref, tiles_ref, out_ref):
    ab = pl.program_id(0)
    tile = tiles_ref.shape[-1]
    out_ref[...] = jnp.zeros(out_ref.shape, out_ref.dtype)

    def place(t, carry):
        i = order_ref[t]
        row = pl.multiple_of(cd_ref[i] * tile, tile)
        out_ref[pl.ds(row, tile), :] = tiles_ref[i]
        return carry

    lax.fori_loop(starts_ref[ab], starts_ref[ab + 1], place, 0)


def _dense_weight(tiles, order, starts, cd_ids, cd_count, ab_count):
    n, tile, _ = tiles.shape
    width = cd_count * tile
    grid_spec = pltpu.PrefetchScalarGridSpec(
        num_scalar_prefetch=3,
        grid=(ab_count,),
        in_specs=[pl.BlockSpec((n, tile, tile), lambda j, *_: (0, 0, 0))],
        out_specs=pl.BlockSpec((width, tile), lambda j, *_: (0, j)),
    )
    return pl.pallas_call(
        _weight_kernel,
        grid_spec=grid_spec,
        out_shape=jax.ShapeDtypeStruct((width, ab_count * tile), tiles.dtype),
        cost_estimate=pl.CostEstimate(
            flops=0, transcendentals=0, bytes_accessed=tiles.size * 2 + width * ab_count * tile * 2
        ),
    )(order, starts, cd_ids, tiles)


class _Halving:
    def __init__(self, partial, bit_order, rep_count):
        self.levels = rep_count.bit_length() - 1
        self.part = partial.shape[0] // rep_count
        self.width = partial.shape[-1]
        self.x = partial.reshape((2,) * self.levels + (self.part, self.width))
        self.axis_bits = list(range(self.levels - 1, -1, -1))
        self.todo = list(bit_order)
        self.rep_count = rep_count

    def advance(self, rep_index):
        if not self.todo:
            return
        bit = self.todo.pop(0)
        ax = self.axis_bits.index(bit)
        mine = (rep_index >> bit) & 1
        keep = lax.dynamic_index_in_dim(self.x, mine, ax, keepdims=False)
        send = lax.dynamic_index_in_dim(self.x, 1 - mine, ax, keepdims=False)
        pairs = [(i, i ^ (1 << bit)) for i in range(self.rep_count)]
        self.x = keep + lax.ppermute(send, "rep", perm=pairs)
        self.axis_bits.pop(ax)

    def result(self):
        return self.x.reshape(self.part, self.width)


def _line_gather(block, own_count):
    me = lax.axis_index("own")
    up = [block]
    down = [block]
    for k in range(1, own_count):
        up.append(lax.ppermute(up[-1], "own", perm=[(i, i + 1) for i in range(k - 1, own_count - 1)]))
        down.append(lax.ppermute(down[-1], "own", perm=[(i + 1, i) for i in range(own_count - k)]))
    out = jnp.zeros((own_count,) + block.shape, block.dtype)
    zero = (0,) * block.ndim
    for k in range(own_count - 1, 0, -1):
        out = lax.dynamic_update_slice(out, up[k][None], (me - k,) + zero)
    for k in range(own_count - 1, 0, -1):
        out = lax.dynamic_update_slice(out, down[k][None], (me + k,) + zero)
    out = lax.dynamic_update_slice(out, block[None], (me,) + zero)
    return out.reshape((own_count * block.shape[0],) + block.shape[1:])


def on_device(amplitudes, integrals, ab_list, cd_list, live_count):
    own_count = lax.axis_size("own")
    rep_count = lax.axis_size("rep")
    peer_count = own_count * rep_count
    slot_count = integrals.shape[0] // peer_count
    received = lax.all_to_all(integrals, ("own", "rep"), split_axis=0, concat_axis=0, tiled=True)
    ab_ids = ab_list.reshape(-1)
    cd_ids = cd_list.reshape(-1)
    live_mask = (
        jnp.arange(slot_count, dtype=jnp.int32)[None, :] < live_count.reshape(peer_count, 1)
    ).reshape(-1)
    order, starts = _slot_order(ab_ids, live_mask, AB_DEV)
    local_rows, width = amplitudes.shape
    tile = integrals.shape[-1]
    subs = rep_count // own_count
    units = sum(CHUNKS)
    part = local_rows // (subs * units)
    local4 = amplitudes.reshape(subs, units, part, width)
    rep_index = lax.axis_index("rep")
    levels = rep_count.bit_length() - 1
    orders = (list(range(levels)), [0] + list(range(levels - 1, 0, -1)))
    bounds = [sum(CHUNKS[:c]) for c in range(len(CHUNKS) + 1)]
    gathered = [lax.all_gather(local4[:, bounds[0]:bounds[1]], "own", axis=0, tiled=True)]
    later, received = lax.optimization_barrier((local4[:, bounds[1]:], received))
    for c in range(1, len(CHUNKS)):
        lo, hi = bounds[c] - bounds[1], bounds[c + 1] - bounds[1]
        gathered.append(_line_gather(later[:, lo:hi], own_count))
    weight = _dense_weight(received, order, starts, cd_ids, width // tile, AB_DEV)
    half = weight.shape[1] // 2
    flows = []
    for chunk in range(len(CHUNKS)):
        for flow in flows:
            flow.advance(rep_index)
        if flows:
            amp4, held = lax.optimization_barrier((gathered[chunk], [f.x for f in flows]))
            for flow, x in zip(flows, held):
                flow.x = x
        else:
            amp4 = gathered[chunk]
        lhs = amp4.reshape(-1, width)
        for h in range(2):
            partial = jnp.dot(lhs, weight[:, h * half:(h + 1) * half], preferred_element_type=jnp.float32)
            flows.append(_Halving(partial, orders[h], rep_count))
    while any(flow.todo for flow in flows):
        for flow in flows:
            flow.advance(rep_index)
    pieces = []
    for chunk in range(len(CHUNKS)):
        size = CHUNKS[chunk]
        sides = [flows[2 * chunk + h].result().reshape(size, part, half) for h in range(2)]
        pieces.append(jnp.concatenate(sides, axis=2))
    return jnp.concatenate(pieces, axis=0).reshape(units * part, 2 * half)


def solution(mesh):
    return jax.shard_map(
        on_device,
        mesh=mesh,
        in_specs=(
            P("own", "rep"),
            P(("own", "rep"), None, None),
            P(("own", "rep"), None, None),
            P(("own", "rep"), None, None),
            P(("own", "rep"), None),
        ),
        out_specs=P("rep", "own"),
        check_vma=False,
    )
```

```python
import functools

import jax
import jax.numpy as jnp
from jax import lax
from jax.experimental import pallas as pl
from jax.experimental.pallas import tpu as pltpu
from jax.sharding import PartitionSpec as P

AB_DEV = 16
N_CHUNK = 4


def _slot_order(ab_ids, live_mask, ab_count):
    n = ab_ids.shape[0]
    key = jnp.where(live_mask, ab_ids, ab_count)
    idx = jnp.arange(n, dtype=jnp.int32)
    earlier = (key[None, :] < key[:, None]) | ((key[None, :] == key[:, None]) & (idx[None, :] < idx[:, None]))
    rank = jnp.sum(earlier.astype(jnp.int32), axis=1)
    order = jnp.sum(jnp.where(rank[None, :] == idx[:, None], idx[None, :], 0), axis=1).astype(jnp.int32)
    bounds = jnp.arange(ab_count + 1, dtype=jnp.int32)
    starts = jnp.sum((key[None, :] < bounds[:, None]).astype(jnp.int32), axis=1).astype(jnp.int32)
    return order, starts


def _ladder_kernel(order_ref, starts_ref, ab_ref, cd_ref, amp_ref, tiles_ref, out_ref, weight_ref):
    step = pl.program_id(0)
    tile = tiles_ref.shape[-1]
    groups, part, width = amp_ref.shape
    per_step = out_ref.shape[1] // tile
    weight_ref[...] = jnp.zeros(weight_ref.shape, weight_ref.dtype)
    first = step * per_step

    def place(t, carry):
        i = order_ref[t]
        row = pl.multiple_of(cd_ref[i] * tile, tile)
        col = pl.multiple_of((ab_ref[i] - first) * tile, tile)
        weight_ref[pl.ds(row, tile), pl.ds(col, tile)] = tiles_ref[i]
        return carry

    lax.fori_loop(starts_ref[first], starts_ref[first + per_step], place, 0)
    lhs = amp_ref[...].reshape(groups * part, width)
    out_ref[...] = jnp.dot(lhs, weight_ref[...], preferred_element_type=jnp.float32)


def _ladder_products(amp3, tiles, order, starts, ab_ids, cd_ids, ab_count):
    groups, part, width = amp3.shape
    rows = groups * part
    n, tile, _ = tiles.shape
    per_step = 2 if ab_count % 2 == 0 else 1
    cost = pl.CostEstimate(
        flops=2 * rows * width * ab_count * tile,
        transcendentals=0,
        bytes_accessed=rows * width * 2 + tiles.size * 2 + rows * ab_count * tile * 4,
    )
    grid_spec = pltpu.PrefetchScalarGridSpec(
        num_scalar_prefetch=4,
        grid=(ab_count // per_step,),
        in_specs=[
            pl.BlockSpec((groups, part, width), lambda j, *_: (0, 0, 0)),
            pl.BlockSpec((n, tile, tile), lambda j, *_: (0, 0, 0)),
        ],
        out_specs=pl.BlockSpec((rows, per_step * tile), lambda j, *_: (0, j)),
        scratch_shapes=[pltpu.VMEM((width, per_step * tile), tiles.dtype)],
    )
    return pl.pallas_call(
        _ladder_kernel,
        grid_spec=grid_spec,
        out_shape=jax.ShapeDtypeStruct((rows, ab_count * tile), jnp.float32),
        cost_estimate=cost,
    )(order, starts, ab_ids, cd_ids, amp3, tiles)


class _Halving:
    def __init__(self, partial, bit_order, rep_count):
        self.levels = rep_count.bit_length() - 1
        self.part = partial.shape[0] // rep_count
        self.width = partial.shape[-1]
        self.x = partial.reshape((2,) * self.levels + (self.part, self.width))
        self.axis_bits = list(range(self.levels - 1, -1, -1))
        self.todo = list(bit_order)
        self.rep_count = rep_count

    def advance(self, rep_index):
        if not self.todo:
            return
        bit = self.todo.pop(0)
        ax = self.axis_bits.index(bit)
        mine = (rep_index >> bit) & 1
        keep = lax.dynamic_index_in_dim(self.x, mine, ax, keepdims=False)
        send = lax.dynamic_index_in_dim(self.x, 1 - mine, ax, keepdims=False)
        pairs = [(i, i ^ (1 << bit)) for i in range(self.rep_count)]
        self.x = keep + lax.ppermute(send, "rep", perm=pairs)
        self.axis_bits.pop(ax)

    def result(self):
        return self.x.reshape(self.part, self.width)


def _line_gather(block, own_count):
    me = lax.axis_index("own")
    up = [block]
    down = [block]
    for k in range(1, own_count):
        up.append(lax.ppermute(up[-1], "own", perm=[(i, i + 1) for i in range(k - 1, own_count - 1)]))
        down.append(lax.ppermute(down[-1], "own", perm=[(i + 1, i) for i in range(own_count - k)]))
    out = jnp.zeros((own_count,) + block.shape, block.dtype)
    zero = (0,) * block.ndim
    for k in range(own_count - 1, 0, -1):
        out = lax.dynamic_update_slice(out, up[k][None], (me - k,) + zero)
    for k in range(own_count - 1, 0, -1):
        out = lax.dynamic_update_slice(out, down[k][None], (me + k,) + zero)
    out = lax.dynamic_update_slice(out, block[None], (me,) + zero)
    return out.reshape((own_count * block.shape[0],) + block.shape[1:])


def on_device(amplitudes, integrals, ab_list, cd_list, live_count):
    own_count = lax.axis_size("own")
    rep_count = lax.axis_size("rep")
    peer_count = own_count * rep_count
    slot_count = integrals.shape[0] // peer_count
    received = lax.all_to_all(integrals, ("own", "rep"), split_axis=0, concat_axis=0, tiled=True)
    ab_ids = ab_list.reshape(-1)
    cd_ids = cd_list.reshape(-1)
    live_mask = (
        jnp.arange(slot_count, dtype=jnp.int32)[None, :] < live_count.reshape(peer_count, 1)
    ).reshape(-1)
    order, starts = _slot_order(ab_ids, live_mask, AB_DEV)
    local_rows, width = amplitudes.shape
    subs = rep_count // own_count
    part = local_rows // (subs * N_CHUNK)
    local4 = amplitudes.reshape(subs, N_CHUNK, part, width)
    rep_index = lax.axis_index("rep")
    levels = rep_count.bit_length() - 1
    orders = (list(range(levels)), [0] + list(range(levels - 1, 0, -1)))
    gathered = [
        lax.all_gather(local4[:, c], "own", axis=0, tiled=True)
        if c < N_CHUNK - 1
        else _line_gather(local4[:, c], own_count)
        for c in range(N_CHUNK)
    ]
    flows = []
    for chunk in range(N_CHUNK):
        for flow in flows:
            flow.advance(rep_index)
        if flows:
            amp3, held = lax.optimization_barrier((gathered[chunk], [f.x for f in flows]))
            for flow, x in zip(flows, held):
                flow.x = x
        else:
            amp3 = gathered[chunk]
        partial = _ladder_products(amp3, received, order, starts, ab_ids, cd_ids, AB_DEV)
        half = partial.shape[1] // 2
        flows.extend(
            _Halving(partial[:, h * half:(h + 1) * half], orders[h], rep_count) for h in range(2)
        )
    while any(flow.todo for flow in flows):
        for flow in flows:
            flow.advance(rep_index)
    pieces = [
        jnp.concatenate([flows[2 * c].result(), flows[2 * c + 1].result()], axis=1)
        for c in range(N_CHUNK)
    ]
    return jnp.concatenate(pieces, axis=0)


def solution(mesh):
    return jax.shard_map(
        on_device,
        mesh=mesh,
        in_specs=(
            P("own", "rep"),
            P(("own", "rep"), None, None),
            P(("own", "rep"), None, None),
            P(("own", "rep"), None, None),
            P(("own", "rep"), None),
        ),
        out_specs=P("rep", "own"),
        check_vma=False,
    )
```

```python
import functools

import jax
import jax.numpy as jnp
from jax import lax
from jax.experimental import pallas as pl
from jax.experimental.pallas import tpu as pltpu
from jax.sharding import PartitionSpec as P

AB_DEV = 16
N_CHUNK = 4


def _slot_order(ab_ids, live_mask, ab_count):
    n = ab_ids.shape[0]
    key = jnp.where(live_mask, ab_ids, ab_count)
    idx = jnp.arange(n, dtype=jnp.int32)
    earlier = (key[None, :] < key[:, None]) | ((key[None, :] == key[:, None]) & (idx[None, :] < idx[:, None]))
    rank = jnp.sum(earlier.astype(jnp.int32), axis=1)
    order = jnp.sum(jnp.where(rank[None, :] == idx[:, None], idx[None, :], 0), axis=1).astype(jnp.int32)
    bounds = jnp.arange(ab_count + 1, dtype=jnp.int32)
    starts = jnp.sum((key[None, :] < bounds[:, None]).astype(jnp.int32), axis=1).astype(jnp.int32)
    return order, starts


def _ladder_kernel(order_ref, starts_ref, ab_ref, cd_ref, amp_ref, tiles_ref, out_ref, weight_ref):
    step = pl.program_id(0)
    tile = tiles_ref.shape[-1]
    groups, part, width = amp_ref.shape
    per_step = out_ref.shape[1] // tile
    weight_ref[...] = jnp.zeros(weight_ref.shape, weight_ref.dtype)
    first = step * per_step

    def place(t, carry):
        i = order_ref[t]
        row = pl.multiple_of(cd_ref[i] * tile, tile)
        col = pl.multiple_of((ab_ref[i] - first) * tile, tile)
        weight_ref[pl.ds(row, tile), pl.ds(col, tile)] = tiles_ref[i]
        return carry

    lax.fori_loop(starts_ref[first], starts_ref[first + per_step], place, 0)
    lhs = amp_ref[...].reshape(groups * part, width)
    out_ref[...] = jnp.dot(lhs, weight_ref[...], preferred_element_type=jnp.float32)


def _ladder_products(amp3, tiles, order, starts, ab_ids, cd_ids, ab_count):
    groups, part, width = amp3.shape
    rows = groups * part
    n, tile, _ = tiles.shape
    per_step = 2 if ab_count % 2 == 0 else 1
    cost = pl.CostEstimate(
        flops=2 * rows * width * ab_count * tile,
        transcendentals=0,
        bytes_accessed=rows * width * 2 + tiles.size * 2 + rows * ab_count * tile * 4,
    )
    grid_spec = pltpu.PrefetchScalarGridSpec(
        num_scalar_prefetch=4,
        grid=(ab_count // per_step,),
        in_specs=[
            pl.BlockSpec((groups, part, width), lambda j, *_: (0, 0, 0)),
            pl.BlockSpec((n, tile, tile), lambda j, *_: (0, 0, 0)),
        ],
        out_specs=pl.BlockSpec((rows, per_step * tile), lambda j, *_: (0, j)),
        scratch_shapes=[pltpu.VMEM((width, per_step * tile), tiles.dtype)],
    )
    return pl.pallas_call(
        _ladder_kernel,
        grid_spec=grid_spec,
        out_shape=jax.ShapeDtypeStruct((rows, ab_count * tile), jnp.float32),
        cost_estimate=cost,
    )(order, starts, ab_ids, cd_ids, amp3, tiles)


class _Halving:
    def __init__(self, partial, bit_order, rep_count):
        self.levels = rep_count.bit_length() - 1
        self.part = partial.shape[0] // rep_count
        self.width = partial.shape[-1]
        self.x = partial.reshape((2,) * self.levels + (self.part, self.width))
        self.axis_bits = list(range(self.levels - 1, -1, -1))
        self.todo = list(bit_order)
        self.rep_count = rep_count

    def advance(self, rep_index):
        if not self.todo:
            return
        bit = self.todo.pop(0)
        ax = self.axis_bits.index(bit)
        mine = (rep_index >> bit) & 1
        keep = lax.dynamic_index_in_dim(self.x, mine, ax, keepdims=False)
        send = lax.dynamic_index_in_dim(self.x, 1 - mine, ax, keepdims=False)
        pairs = [(i, i ^ (1 << bit)) for i in range(self.rep_count)]
        self.x = keep + lax.ppermute(send, "rep", perm=pairs)
        self.axis_bits.pop(ax)

    def result(self):
        return self.x.reshape(self.part, self.width)


def on_device(amplitudes, integrals, ab_list, cd_list, live_count):
    own_count = lax.axis_size("own")
    rep_count = lax.axis_size("rep")
    peer_count = own_count * rep_count
    slot_count = integrals.shape[0] // peer_count
    received = lax.all_to_all(integrals, ("own", "rep"), split_axis=0, concat_axis=0, tiled=True)
    ab_ids = ab_list.reshape(-1)
    cd_ids = cd_list.reshape(-1)
    live_mask = (
        jnp.arange(slot_count, dtype=jnp.int32)[None, :] < live_count.reshape(peer_count, 1)
    ).reshape(-1)
    order, starts = _slot_order(ab_ids, live_mask, AB_DEV)
    local_rows, width = amplitudes.shape
    subs = rep_count // own_count
    part = local_rows // (subs * N_CHUNK)
    local4 = amplitudes.reshape(subs, N_CHUNK, part, width)
    rep_index = lax.axis_index("rep")
    levels = rep_count.bit_length() - 1
    orders = (list(range(levels)), [0] + list(range(levels - 1, 0, -1)))
    gathered = [lax.all_gather(local4[:, c], "own", axis=0, tiled=True) for c in range(N_CHUNK - 1)]
    last = local4[:, N_CHUNK - 1]
    copies = jnp.broadcast_to(last[None], (own_count,) + last.shape)
    gathered.append(
        lax.all_to_all(copies, "own", split_axis=0, concat_axis=0, tiled=True).reshape(
            (own_count * last.shape[0],) + last.shape[1:]
        )
    )
    flows = []
    for chunk in range(N_CHUNK):
        for flow in flows:
            flow.advance(rep_index)
        if flows:
            amp3, held = lax.optimization_barrier((gathered[chunk], [f.x for f in flows]))
            for flow, x in zip(flows, held):
                flow.x = x
        else:
            amp3 = gathered[chunk]
        partial = _ladder_products(amp3, received, order, starts, ab_ids, cd_ids, AB_DEV)
        half = partial.shape[1] // 2
        flows.extend(
            _Halving(partial[:, h * half:(h + 1) * half], orders[h], rep_count) for h in range(2)
        )
    while any(flow.todo for flow in flows):
        for flow in flows:
            flow.advance(rep_index)
    pieces = [
        jnp.concatenate([flows[2 * c].result(), flows[2 * c + 1].result()], axis=1)
        for c in range(N_CHUNK)
    ]
    return jnp.concatenate(pieces, axis=0)


def solution(mesh):
    return jax.shard_map(
        on_device,
        mesh=mesh,
        in_specs=(
            P("own", "rep"),
            P(("own", "rep"), None, None),
            P(("own", "rep"), None, None),
            P(("own", "rep"), None, None),
            P(("own", "rep"), None),
        ),
        out_specs=P("rep", "own"),
        check_vma=False,
    )
```

```python
import functools

import jax
import jax.numpy as jnp
from jax import lax
from jax.experimental import pallas as pl
from jax.experimental.pallas import tpu as pltpu
from jax.sharding import PartitionSpec as P

AB_DEV = 16
N_CHUNK = 4


def _slot_order(ab_ids, live_mask, ab_count):
    n = ab_ids.shape[0]
    key = jnp.where(live_mask, ab_ids, ab_count)
    idx = jnp.arange(n, dtype=jnp.int32)
    earlier = (key[None, :] < key[:, None]) | ((key[None, :] == key[:, None]) & (idx[None, :] < idx[:, None]))
    rank = jnp.sum(earlier.astype(jnp.int32), axis=1)
    order = jnp.sum(jnp.where(rank[None, :] == idx[:, None], idx[None, :], 0), axis=1).astype(jnp.int32)
    bounds = jnp.arange(ab_count + 1, dtype=jnp.int32)
    starts = jnp.sum((key[None, :] < bounds[:, None]).astype(jnp.int32), axis=1).astype(jnp.int32)
    return order, starts


def _ladder_kernel(order_ref, starts_ref, ab_ref, cd_ref, amp_ref, tiles_ref, out_ref, weight_ref):
    step = pl.program_id(0)
    tile = tiles_ref.shape[-1]
    groups, part, width = amp_ref.shape
    per_step = out_ref.shape[1] // tile
    weight_ref[...] = jnp.zeros(weight_ref.shape, weight_ref.dtype)
    first = step * per_step

    def place(t, carry):
        i = order_ref[t]
        row = pl.multiple_of(cd_ref[i] * tile, tile)
        col = pl.multiple_of((ab_ref[i] - first) * tile, tile)
        weight_ref[pl.ds(row, tile), pl.ds(col, tile)] = tiles_ref[i]
        return carry

    lax.fori_loop(starts_ref[first], starts_ref[first + per_step], place, 0)
    lhs = amp_ref[...].reshape(groups * part, width)
    out_ref[...] = jnp.dot(lhs, weight_ref[...], preferred_element_type=jnp.float32)


def _ladder_products(amp3, tiles, order, starts, ab_ids, cd_ids, ab_count):
    groups, part, width = amp3.shape
    rows = groups * part
    n, tile, _ = tiles.shape
    per_step = 2 if ab_count % 2 == 0 else 1
    cost = pl.CostEstimate(
        flops=2 * rows * width * ab_count * tile,
        transcendentals=0,
        bytes_accessed=rows * width * 2 + tiles.size * 2 + rows * ab_count * tile * 4,
    )
    grid_spec = pltpu.PrefetchScalarGridSpec(
        num_scalar_prefetch=4,
        grid=(ab_count // per_step,),
        in_specs=[
            pl.BlockSpec((groups, part, width), lambda j, *_: (0, 0, 0)),
            pl.BlockSpec((n, tile, tile), lambda j, *_: (0, 0, 0)),
        ],
        out_specs=pl.BlockSpec((rows, per_step * tile), lambda j, *_: (0, j)),
        scratch_shapes=[pltpu.VMEM((width, per_step * tile), tiles.dtype)],
    )
    return pl.pallas_call(
        _ladder_kernel,
        grid_spec=grid_spec,
        out_shape=jax.ShapeDtypeStruct((rows, ab_count * tile), jnp.float32),
        cost_estimate=cost,
    )(order, starts, ab_ids, cd_ids, amp3, tiles)


class _Halving:
    def __init__(self, partial, bit_order, rep_count):
        self.levels = rep_count.bit_length() - 1
        self.part = partial.shape[0] // rep_count
        self.width = partial.shape[-1]
        self.x = partial.reshape((2,) * self.levels + (self.part, self.width))
        self.axis_bits = list(range(self.levels - 1, -1, -1))
        self.todo = list(bit_order)
        self.rep_count = rep_count

    def advance(self, rep_index):
        if not self.todo:
            return
        bit = self.todo.pop(0)
        ax = self.axis_bits.index(bit)
        mine = (rep_index >> bit) & 1
        keep = lax.dynamic_index_in_dim(self.x, mine, ax, keepdims=False)
        send = lax.dynamic_index_in_dim(self.x, 1 - mine, ax, keepdims=False)
        pairs = [(i, i ^ (1 << bit)) for i in range(self.rep_count)]
        self.x = keep + lax.ppermute(send, "rep", perm=pairs)
        self.axis_bits.pop(ax)

    def result(self):
        return self.x.reshape(self.part, self.width)


def on_device(amplitudes, integrals, ab_list, cd_list, live_count):
    own_count = lax.axis_size("own")
    rep_count = lax.axis_size("rep")
    peer_count = own_count * rep_count
    slot_count = integrals.shape[0] // peer_count
    received = lax.all_to_all(integrals, ("own", "rep"), split_axis=0, concat_axis=0, tiled=True)
    ab_ids = ab_list.reshape(-1)
    cd_ids = cd_list.reshape(-1)
    live_mask = (
        jnp.arange(slot_count, dtype=jnp.int32)[None, :] < live_count.reshape(peer_count, 1)
    ).reshape(-1)
    order, starts = _slot_order(ab_ids, live_mask, AB_DEV)
    local_rows, width = amplitudes.shape
    subs = rep_count // own_count
    part = local_rows // (subs * N_CHUNK)
    local4 = amplitudes.reshape(subs, N_CHUNK, part, width)
    rep_index = lax.axis_index("rep")
    levels = rep_count.bit_length() - 1
    orders = (list(range(levels)), [0] + list(range(levels - 1, 0, -1)))
    gathered = [lax.all_gather(local4[:, c], "own", axis=0, tiled=True) for c in range(N_CHUNK - 1)]
    last = local4[:, N_CHUNK - 1]
    copies = jnp.broadcast_to(last[None], (own_count,) + last.shape)
    gathered.append(
        lax.all_to_all(copies, "own", split_axis=0, concat_axis=0, tiled=True).reshape(
            (own_count * last.shape[0],) + last.shape[1:]
        )
    )
    flows = {}
    sequence = list(range(N_CHUNK - 2)) + [N_CHUNK - 1, N_CHUNK - 2]
    for chunk in sequence:
        active = [flow for pair in flows.values() for flow in pair]
        for flow in active:
            flow.advance(rep_index)
        if active:
            amp3, held = lax.optimization_barrier((gathered[chunk], [f.x for f in active]))
            for flow, x in zip(active, held):
                flow.x = x
        else:
            amp3 = gathered[chunk]
        partial = _ladder_products(amp3, received, order, starts, ab_ids, cd_ids, AB_DEV)
        half = partial.shape[1] // 2
        flows[chunk] = [
            _Halving(partial[:, h * half:(h + 1) * half], orders[h], rep_count) for h in range(2)
        ]
    active = [flow for pair in flows.values() for flow in pair]
    while any(flow.todo for flow in active):
        for flow in active:
            flow.advance(rep_index)
    pieces = [
        jnp.concatenate([flows[c][0].result(), flows[c][1].result()], axis=1) for c in range(N_CHUNK)
    ]
    return jnp.concatenate(pieces, axis=0)


def solution(mesh):
    return jax.shard_map(
        on_device,
        mesh=mesh,
        in_specs=(
            P("own", "rep"),
            P(("own", "rep"), None, None),
            P(("own", "rep"), None, None),
            P(("own", "rep"), None, None),
            P(("own", "rep"), None),
        ),
        out_specs=P("rep", "own"),
        check_vma=False,
    )
```

```python
import functools

import jax
import jax.numpy as jnp
from jax import lax
from jax.experimental import pallas as pl
from jax.experimental.pallas import tpu as pltpu
from jax.sharding import PartitionSpec as P

AB_DEV = 16
CHUNKS = (1, 1, 1, 1)


def _slot_order(ab_ids, live_mask, ab_count):
    n = ab_ids.shape[0]
    key = jnp.where(live_mask, ab_ids, ab_count)
    idx = jnp.arange(n, dtype=jnp.int32)
    earlier = (key[None, :] < key[:, None]) | ((key[None, :] == key[:, None]) & (idx[None, :] < idx[:, None]))
    rank = jnp.sum(earlier.astype(jnp.int32), axis=1)
    order = jnp.sum(jnp.where(rank[None, :] == idx[:, None], idx[None, :], 0), axis=1).astype(jnp.int32)
    bounds = jnp.arange(ab_count + 1, dtype=jnp.int32)
    starts = jnp.sum((key[None, :] < bounds[:, None]).astype(jnp.int32), axis=1).astype(jnp.int32)
    return order, starts


def _weight_kernel(order_ref, starts_ref, cd_ref, tiles_ref, out_ref):
    ab = pl.program_id(0)
    tile = tiles_ref.shape[-1]
    out_ref[...] = jnp.zeros(out_ref.shape, out_ref.dtype)

    def place(t, carry):
        i = order_ref[t]
        row = pl.multiple_of(cd_ref[i] * tile, tile)
        out_ref[pl.ds(row, tile), :] = tiles_ref[i]
        return carry

    lax.fori_loop(starts_ref[ab], starts_ref[ab + 1], place, 0)


def _dense_weight(tiles, order, starts, cd_ids, cd_count, ab_count):
    n, tile, _ = tiles.shape
    width = cd_count * tile
    grid_spec = pltpu.PrefetchScalarGridSpec(
        num_scalar_prefetch=3,
        grid=(ab_count,),
        in_specs=[pl.BlockSpec((n, tile, tile), lambda j, *_: (0, 0, 0))],
        out_specs=pl.BlockSpec((width, tile), lambda j, *_: (0, j)),
    )
    return pl.pallas_call(
        _weight_kernel,
        grid_spec=grid_spec,
        out_shape=jax.ShapeDtypeStruct((width, ab_count * tile), tiles.dtype),
        cost_estimate=pl.CostEstimate(
            flops=0, transcendentals=0, bytes_accessed=tiles.size * 2 + width * ab_count * tile * 2
        ),
    )(order, starts, cd_ids, tiles)


class _Halving:
    def __init__(self, partial, bit_order, rep_count):
        self.levels = rep_count.bit_length() - 1
        self.part = partial.shape[0] // rep_count
        self.width = partial.shape[-1]
        self.x = partial.reshape((2,) * self.levels + (self.part, self.width))
        self.axis_bits = list(range(self.levels - 1, -1, -1))
        self.todo = list(bit_order)
        self.rep_count = rep_count

    def advance(self, rep_index):
        if not self.todo:
            return
        bit = self.todo.pop(0)
        ax = self.axis_bits.index(bit)
        mine = (rep_index >> bit) & 1
        keep = lax.dynamic_index_in_dim(self.x, mine, ax, keepdims=False)
        send = lax.dynamic_index_in_dim(self.x, 1 - mine, ax, keepdims=False)
        pairs = [(i, i ^ (1 << bit)) for i in range(self.rep_count)]
        self.x = keep + lax.ppermute(send, "rep", perm=pairs)
        self.axis_bits.pop(ax)

    def result(self):
        return self.x.reshape(self.part, self.width)


def on_device(amplitudes, integrals, ab_list, cd_list, live_count):
    own_count = lax.axis_size("own")
    rep_count = lax.axis_size("rep")
    peer_count = own_count * rep_count
    slot_count = integrals.shape[0] // peer_count
    received = lax.all_to_all(integrals, ("own", "rep"), split_axis=0, concat_axis=0, tiled=True)
    ab_ids = ab_list.reshape(-1)
    cd_ids = cd_list.reshape(-1)
    live_mask = (
        jnp.arange(slot_count, dtype=jnp.int32)[None, :] < live_count.reshape(peer_count, 1)
    ).reshape(-1)
    order, starts = _slot_order(ab_ids, live_mask, AB_DEV)
    local_rows, width = amplitudes.shape
    tile = integrals.shape[-1]
    weight = _dense_weight(received, order, starts, cd_ids, width // tile, AB_DEV)
    subs = rep_count // own_count
    units = sum(CHUNKS)
    part = local_rows // (subs * units)
    local4 = amplitudes.reshape(subs, units, part, width)
    rep_index = lax.axis_index("rep")
    levels = rep_count.bit_length() - 1
    orders = (list(range(levels)), [0] + list(range(levels - 1, 0, -1)))
    bounds = [sum(CHUNKS[:c]) for c in range(len(CHUNKS) + 1)]
    gathered = [
        lax.all_gather(local4[:, bounds[c]:bounds[c + 1]], "own", axis=0, tiled=True)
        for c in range(len(CHUNKS))
    ]
    half = weight.shape[1] // 2
    flows = []
    for chunk in range(len(CHUNKS)):
        for flow in flows:
            flow.advance(rep_index)
        if flows:
            amp4, held = lax.optimization_barrier((gathered[chunk], [f.x for f in flows]))
            for flow, x in zip(flows, held):
                flow.x = x
        else:
            amp4 = gathered[chunk]
        lhs = amp4.reshape(-1, width)
        for h in range(2):
            partial = jnp.dot(lhs, weight[:, h * half:(h + 1) * half], preferred_element_type=jnp.float32)
            flows.append(_Halving(partial, orders[h], rep_count))
    while any(flow.todo for flow in flows):
        for flow in flows:
            flow.advance(rep_index)
    pieces = []
    for chunk in range(len(CHUNKS)):
        size = CHUNKS[chunk]
        sides = [flows[2 * chunk + h].result().reshape(size, part, half) for h in range(2)]
        pieces.append(jnp.concatenate(sides, axis=2))
    return jnp.concatenate(pieces, axis=0).reshape(units * part, 2 * half)


def solution(mesh):
    return jax.shard_map(
        on_device,
        mesh=mesh,
        in_specs=(
            P("own", "rep"),
            P(("own", "rep"), None, None),
            P(("own", "rep"), None, None),
            P(("own", "rep"), None, None),
            P(("own", "rep"), None),
        ),
        out_specs=P("rep", "own"),
        check_vma=False,
    )
```

```python
import functools

import jax
import jax.numpy as jnp
from jax import lax
from jax.experimental import pallas as pl
from jax.experimental.pallas import tpu as pltpu
from jax.sharding import PartitionSpec as P

AB_DEV = 16
CHUNKS = (1, 1, 1, 1)


def _slot_order(ab_ids, live_mask, ab_count):
    n = ab_ids.shape[0]
    key = jnp.where(live_mask, ab_ids, ab_count)
    idx = jnp.arange(n, dtype=jnp.int32)
    earlier = (key[None, :] < key[:, None]) | ((key[None, :] == key[:, None]) & (idx[None, :] < idx[:, None]))
    rank = jnp.sum(earlier.astype(jnp.int32), axis=1)
    order = jnp.sum(jnp.where(rank[None, :] == idx[:, None], idx[None, :], 0), axis=1).astype(jnp.int32)
    bounds = jnp.arange(ab_count + 1, dtype=jnp.int32)
    starts = jnp.sum((key[None, :] < bounds[:, None]).astype(jnp.int32), axis=1).astype(jnp.int32)
    return order, starts


def _weight_kernel(order_ref, starts_ref, cd_ref, tiles_ref, out_ref):
    ab = pl.program_id(0)
    tile = tiles_ref.shape[-1]
    out_ref[...] = jnp.zeros(out_ref.shape, out_ref.dtype)

    def place(t, carry):
        i = order_ref[t]
        row = pl.multiple_of(cd_ref[i] * tile, tile)
        out_ref[pl.ds(row, tile), :] = tiles_ref[i]
        return carry

    lax.fori_loop(starts_ref[ab], starts_ref[ab + 1], place, 0)


def _dense_weight(tiles, order, starts, cd_ids, cd_count, ab_count):
    n, tile, _ = tiles.shape
    width = cd_count * tile
    grid_spec = pltpu.PrefetchScalarGridSpec(
        num_scalar_prefetch=3,
        grid=(ab_count,),
        in_specs=[pl.BlockSpec((n, tile, tile), lambda j, *_: (0, 0, 0))],
        out_specs=pl.BlockSpec((width, tile), lambda j, *_: (0, j)),
    )
    return pl.pallas_call(
        _weight_kernel,
        grid_spec=grid_spec,
        out_shape=jax.ShapeDtypeStruct((width, ab_count * tile), tiles.dtype),
        cost_estimate=pl.CostEstimate(
            flops=0, transcendentals=0, bytes_accessed=tiles.size * 2 + width * ab_count * tile * 2
        ),
    )(order, starts, cd_ids, tiles)


class _Halving:
    def __init__(self, partial, bit_order, rep_count):
        self.levels = rep_count.bit_length() - 1
        self.part = partial.shape[0] // rep_count
        self.width = partial.shape[-1]
        self.x = partial.reshape((2,) * self.levels + (self.part, self.width))
        self.axis_bits = list(range(self.levels - 1, -1, -1))
        self.todo = list(bit_order)
        self.rep_count = rep_count

    def advance(self, rep_index):
        if not self.todo:
            return
        bit = self.todo.pop(0)
        ax = self.axis_bits.index(bit)
        mine = (rep_index >> bit) & 1
        keep = lax.dynamic_index_in_dim(self.x, mine, ax, keepdims=False)
        send = lax.dynamic_index_in_dim(self.x, 1 - mine, ax, keepdims=False)
        pairs = [(i, i ^ (1 << bit)) for i in range(self.rep_count)]
        self.x = keep + lax.ppermute(send, "rep", perm=pairs)
        self.axis_bits.pop(ax)

    def result(self):
        return self.x.reshape(self.part, self.width)


def on_device(amplitudes, integrals, ab_list, cd_list, live_count):
    own_count = lax.axis_size("own")
    rep_count = lax.axis_size("rep")
    peer_count = own_count * rep_count
    slot_count = integrals.shape[0] // peer_count
    received = lax.all_to_all(integrals, ("own", "rep"), split_axis=0, concat_axis=0, tiled=True)
    ab_ids = ab_list.reshape(-1)
    cd_ids = cd_list.reshape(-1)
    live_mask = (
        jnp.arange(slot_count, dtype=jnp.int32)[None, :] < live_count.reshape(peer_count, 1)
    ).reshape(-1)
    order, starts = _slot_order(ab_ids, live_mask, AB_DEV)
    local_rows, width = amplitudes.shape
    tile = integrals.shape[-1]
    weight = _dense_weight(received, order, starts, cd_ids, width // tile, AB_DEV)
    subs = rep_count // own_count
    units = sum(CHUNKS)
    part = local_rows // (subs * units)
    local4 = amplitudes.reshape(subs, units, part, width)
    rep_index = lax.axis_index("rep")
    levels = rep_count.bit_length() - 1
    orders = (list(range(levels)), [0] + list(range(levels - 1, 0, -1)))
    bounds = [sum(CHUNKS[:c]) for c in range(len(CHUNKS) + 1)]
    gathered = [
        lax.all_gather(local4[:, bounds[c]:bounds[c + 1]], "own", axis=0, tiled=True)
        for c in range(len(CHUNKS))
    ]
    half = weight.shape[1] // 2
    flows = []
    for chunk in range(len(CHUNKS)):
        rounds = 1 if chunk < len(CHUNKS) - 1 else levels
        for _ in range(rounds):
            for flow in flows:
                flow.advance(rep_index)
        if flows:
            amp4, held = lax.optimization_barrier((gathered[chunk], [f.x for f in flows]))
            for flow, x in zip(flows, held):
                flow.x = x
        else:
            amp4 = gathered[chunk]
        lhs = amp4.reshape(-1, width)
        for h in range(2):
            partial = jnp.dot(lhs, weight[:, h * half:(h + 1) * half], preferred_element_type=jnp.float32)
            flows.append(_Halving(partial, orders[h], rep_count))
    while any(flow.todo for flow in flows):
        for flow in flows:
            flow.advance(rep_index)
    pieces = []
    for chunk in range(len(CHUNKS)):
        size = CHUNKS[chunk]
        sides = [flows[2 * chunk + h].result().reshape(size, part, half) for h in range(2)]
        pieces.append(jnp.concatenate(sides, axis=2))
    return jnp.concatenate(pieces, axis=0).reshape(units * part, 2 * half)


def solution(mesh):
    return jax.shard_map(
        on_device,
        mesh=mesh,
        in_specs=(
            P("own", "rep"),
            P(("own", "rep"), None, None),
            P(("own", "rep"), None, None),
            P(("own", "rep"), None, None),
            P(("own", "rep"), None),
        ),
        out_specs=P("rep", "own"),
        check_vma=False,
    )
```

```python
import functools

import jax
import jax.numpy as jnp
from jax import lax
from jax.experimental import pallas as pl
from jax.experimental.pallas import tpu as pltpu
from jax.sharding import PartitionSpec as P

AB_DEV = 16
CHUNKS = (1, 1, 1, 1)


def _slot_order(ab_ids, live_mask, ab_count):
    n = ab_ids.shape[0]
    key = jnp.where(live_mask, ab_ids, ab_count)
    idx = jnp.arange(n, dtype=jnp.int32)
    earlier = (key[None, :] < key[:, None]) | ((key[None, :] == key[:, None]) & (idx[None, :] < idx[:, None]))
    rank = jnp.sum(earlier.astype(jnp.int32), axis=1)
    order = jnp.sum(jnp.where(rank[None, :] == idx[:, None], idx[None, :], 0), axis=1).astype(jnp.int32)
    bounds = jnp.arange(ab_count + 1, dtype=jnp.int32)
    starts = jnp.sum((key[None, :] < bounds[:, None]).astype(jnp.int32), axis=1).astype(jnp.int32)
    return order, starts


def _weight_kernel(order_ref, starts_ref, cd_ref, tiles_ref, out_ref):
    ab = pl.program_id(0)
    tile = tiles_ref.shape[-1]
    out_ref[...] = jnp.zeros(out_ref.shape, out_ref.dtype)

    def place(t, carry):
        i = order_ref[t]
        row = pl.multiple_of(cd_ref[i] * tile, tile)
        out_ref[pl.ds(row, tile), :] = tiles_ref[i]
        return carry

    lax.fori_loop(starts_ref[ab], starts_ref[ab + 1], place, 0)


def _dense_weight(tiles, order, starts, cd_ids, cd_count, ab_count):
    n, tile, _ = tiles.shape
    width = cd_count * tile
    grid_spec = pltpu.PrefetchScalarGridSpec(
        num_scalar_prefetch=3,
        grid=(ab_count,),
        in_specs=[pl.BlockSpec((n, tile, tile), lambda j, *_: (0, 0, 0))],
        out_specs=pl.BlockSpec((width, tile), lambda j, *_: (0, j)),
    )
    return pl.pallas_call(
        _weight_kernel,
        grid_spec=grid_spec,
        out_shape=jax.ShapeDtypeStruct((width, ab_count * tile), tiles.dtype),
        cost_estimate=pl.CostEstimate(
            flops=0, transcendentals=0, bytes_accessed=tiles.size * 2 + width * ab_count * tile * 2
        ),
    )(order, starts, cd_ids, tiles)


class _Halving:
    def __init__(self, partial, bit_order, rep_count):
        self.levels = rep_count.bit_length() - 1
        self.part = partial.shape[0] // rep_count
        self.width = partial.shape[-1]
        self.x = partial.reshape((2,) * self.levels + (self.part, self.width))
        self.axis_bits = list(range(self.levels - 1, -1, -1))
        self.todo = list(bit_order)
        self.rep_count = rep_count

    def advance(self, rep_index):
        if not self.todo:
            return
        bit = self.todo.pop(0)
        ax = self.axis_bits.index(bit)
        mine = (rep_index >> bit) & 1
        keep = lax.dynamic_index_in_dim(self.x, mine, ax, keepdims=False)
        send = lax.dynamic_index_in_dim(self.x, 1 - mine, ax, keepdims=False)
        pairs = [(i, i ^ (1 << bit)) for i in range(self.rep_count)]
        self.x = keep + lax.ppermute(send, "rep", perm=pairs)
        self.axis_bits.pop(ax)

    def result(self):
        return self.x.reshape(self.part, self.width)


def on_device(amplitudes, integrals, ab_list, cd_list, live_count):
    own_count = lax.axis_size("own")
    rep_count = lax.axis_size("rep")
    peer_count = own_count * rep_count
    slot_count = integrals.shape[0] // peer_count
    received = lax.all_to_all(integrals, ("own", "rep"), split_axis=0, concat_axis=0, tiled=True)
    ab_ids = ab_list.reshape(-1)
    cd_ids = cd_list.reshape(-1)
    live_mask = (
        jnp.arange(slot_count, dtype=jnp.int32)[None, :] < live_count.reshape(peer_count, 1)
    ).reshape(-1)
    order, starts = _slot_order(ab_ids, live_mask, AB_DEV)
    local_rows, width = amplitudes.shape
    tile = integrals.shape[-1]
    weight = _dense_weight(received, order, starts, cd_ids, width // tile, AB_DEV)
    subs = rep_count // own_count
    units = sum(CHUNKS)
    part = local_rows // (subs * units)
    local4 = amplitudes.reshape(subs, units, part, width)
    rep_index = lax.axis_index("rep")
    levels = rep_count.bit_length() - 1
    orders = (list(range(levels)), [0] + list(range(levels - 1, 0, -1)))
    bounds = [sum(CHUNKS[:c]) for c in range(len(CHUNKS) + 1)]
    gathered = [
        lax.all_gather(local4[:, bounds[c]:bounds[c + 1]], "own", axis=0, tiled=True)
        for c in range(len(CHUNKS))
    ]
    half = weight.shape[1] // 2
    flows = []
    for chunk in range(len(CHUNKS)):
        if flows:
            amp4, held = lax.optimization_barrier((gathered[chunk], [f.x for f in flows]))
            for flow, x in zip(flows, held):
                flow.x = x
        else:
            amp4 = gathered[chunk]
        for flow in flows:
            flow.advance(rep_index)
        lhs = amp4.reshape(-1, width)
        for h in range(2):
            partial = jnp.dot(lhs, weight[:, h * half:(h + 1) * half], preferred_element_type=jnp.float32)
            flows.append(_Halving(partial, orders[h], rep_count))
    while any(flow.todo for flow in flows):
        for flow in flows:
            flow.advance(rep_index)
    pieces = []
    for chunk in range(len(CHUNKS)):
        size = CHUNKS[chunk]
        sides = [flows[2 * chunk + h].result().reshape(size, part, half) for h in range(2)]
        pieces.append(jnp.concatenate(sides, axis=2))
    return jnp.concatenate(pieces, axis=0).reshape(units * part, 2 * half)


def solution(mesh):
    return jax.shard_map(
        on_device,
        mesh=mesh,
        in_specs=(
            P("own", "rep"),
            P(("own", "rep"), None, None),
            P(("own", "rep"), None, None),
            P(("own", "rep"), None, None),
            P(("own", "rep"), None),
        ),
        out_specs=P("rep", "own"),
        check_vma=False,
    )
```

```python
import functools

import jax
import jax.numpy as jnp
from jax import lax
from jax.experimental import pallas as pl
from jax.experimental.pallas import tpu as pltpu
from jax.sharding import PartitionSpec as P

AB_DEV = 16
N_CHUNK = 4


def _slot_order(ab_ids, live_mask, ab_count):
    n = ab_ids.shape[0]
    key = jnp.where(live_mask, ab_ids, ab_count)
    idx = jnp.arange(n, dtype=jnp.int32)
    earlier = (key[None, :] < key[:, None]) | ((key[None, :] == key[:, None]) & (idx[None, :] < idx[:, None]))
    rank = jnp.sum(earlier.astype(jnp.int32), axis=1)
    order = jnp.sum(jnp.where(rank[None, :] == idx[:, None], idx[None, :], 0), axis=1).astype(jnp.int32)
    bounds = jnp.arange(ab_count + 1, dtype=jnp.int32)
    starts = jnp.sum((key[None, :] < bounds[:, None]).astype(jnp.int32), axis=1).astype(jnp.int32)
    return order, starts


def _ladder_kernel(order_ref, starts_ref, ab_ref, cd_ref, amp_ref, tiles_ref, out_ref, weight_ref):
    step = pl.program_id(0)
    tile = tiles_ref.shape[-1]
    groups, part, width = amp_ref.shape
    per_step = out_ref.shape[-1] // tile
    weight_ref[...] = jnp.zeros(weight_ref.shape, weight_ref.dtype)
    first = step * per_step

    def place(t, carry):
        i = order_ref[t]
        row = pl.multiple_of(cd_ref[i] * tile, tile)
        col = pl.multiple_of((ab_ref[i] - first) * tile, tile)
        weight_ref[pl.ds(row, tile), pl.ds(col, tile)] = tiles_ref[i]
        return carry

    lax.fori_loop(starts_ref[first], starts_ref[first + per_step], place, 0)
    lhs = amp_ref[...].reshape(groups * part, width)
    out_ref[...] = jnp.dot(lhs, weight_ref[...], preferred_element_type=jnp.float32)


def _ladder_products(amp3, tiles, order, starts, ab_ids, cd_ids, ab_count):
    groups, part, width = amp3.shape
    rows = groups * part
    n, tile, _ = tiles.shape
    per_step = 4 if ab_count % 8 == 0 else 1
    steps_per_half = ab_count // (2 * per_step)
    cost = pl.CostEstimate(
        flops=2 * rows * width * ab_count * tile,
        transcendentals=0,
        bytes_accessed=rows * width * 2 + tiles.size * 2 + rows * ab_count * tile * 4,
    )
    grid_spec = pltpu.PrefetchScalarGridSpec(
        num_scalar_prefetch=4,
        grid=(ab_count // per_step,),
        in_specs=[
            pl.BlockSpec((groups, part, width), lambda j, *_: (0, 0, 0)),
            pl.BlockSpec((n, tile, tile), lambda j, *_: (0, 0, 0)),
        ],
        out_specs=pl.BlockSpec(
            (None, rows, per_step * tile), lambda j, *_: (j // steps_per_half, 0, j % steps_per_half)
        ),
        scratch_shapes=[pltpu.VMEM((width, per_step * tile), tiles.dtype)],
    )
    return pl.pallas_call(
        _ladder_kernel,
        grid_spec=grid_spec,
        out_shape=jax.ShapeDtypeStruct((2, rows, ab_count * tile // 2), jnp.float32),
        cost_estimate=cost,
    )(order, starts, ab_ids, cd_ids, amp3, tiles)


class _Halving:
    def __init__(self, partial, bit_order, rep_count):
        self.levels = rep_count.bit_length() - 1
        self.part = partial.shape[0] // rep_count
        self.width = partial.shape[-1]
        self.x = partial.reshape((2,) * self.levels + (self.part, self.width))
        self.axis_bits = list(range(self.levels - 1, -1, -1))
        self.todo = list(bit_order)
        self.rep_count = rep_count

    def advance(self, rep_index):
        if not self.todo:
            return
        bit = self.todo.pop(0)
        ax = self.axis_bits.index(bit)
        mine = (rep_index >> bit) & 1
        keep = lax.dynamic_index_in_dim(self.x, mine, ax, keepdims=False)
        send = lax.dynamic_index_in_dim(self.x, 1 - mine, ax, keepdims=False)
        pairs = [(i, i ^ (1 << bit)) for i in range(self.rep_count)]
        self.x = keep + lax.ppermute(send, "rep", perm=pairs)
        self.axis_bits.pop(ax)

    def result(self):
        return self.x.reshape(self.part, self.width)


def on_device(amplitudes, integrals, ab_list, cd_list, live_count):
    own_count = lax.axis_size("own")
    rep_count = lax.axis_size("rep")
    peer_count = own_count * rep_count
    slot_count = integrals.shape[0] // peer_count
    received = lax.all_to_all(integrals, ("own", "rep"), split_axis=0, concat_axis=0, tiled=True)
    ab_ids = ab_list.reshape(-1)
    cd_ids = cd_list.reshape(-1)
    live_mask = (
        jnp.arange(slot_count, dtype=jnp.int32)[None, :] < live_count.reshape(peer_count, 1)
    ).reshape(-1)
    order, starts = _slot_order(ab_ids, live_mask, AB_DEV)
    local_rows, width = amplitudes.shape
    subs = rep_count // own_count
    part = local_rows // (subs * N_CHUNK)
    local4 = amplitudes.reshape(subs, N_CHUNK, part, width)
    rep_index = lax.axis_index("rep")
    levels = rep_count.bit_length() - 1
    orders = (list(range(levels)), [0] + list(range(levels - 1, 0, -1)))
    gathered = [lax.all_gather(local4[:, c], "own", axis=0, tiled=True) for c in range(N_CHUNK)]
    flows = []
    for chunk in range(N_CHUNK):
        for flow in flows:
            flow.advance(rep_index)
        if flows:
            amp3, held = lax.optimization_barrier((gathered[chunk], [f.x for f in flows]))
            for flow, x in zip(flows, held):
                flow.x = x
        else:
            amp3 = gathered[chunk]
        partial = _ladder_products(amp3, received, order, starts, ab_ids, cd_ids, AB_DEV)
        flows.extend(_Halving(partial[h], orders[h], rep_count) for h in range(2))
    while any(flow.todo for flow in flows):
        for flow in flows:
            flow.advance(rep_index)
    pieces = [
        jnp.concatenate([flows[2 * c].result(), flows[2 * c + 1].result()], axis=1)
        for c in range(N_CHUNK)
    ]
    return jnp.concatenate(pieces, axis=0)


def solution(mesh):
    return jax.shard_map(
        on_device,
        mesh=mesh,
        in_specs=(
            P("own", "rep"),
            P(("own", "rep"), None, None),
            P(("own", "rep"), None, None),
            P(("own", "rep"), None, None),
            P(("own", "rep"), None),
        ),
        out_specs=P("rep", "own"),
        check_vma=False,
    )
```

```python
import functools

import jax
import jax.numpy as jnp
from jax import lax
from jax.experimental import pallas as pl
from jax.experimental.pallas import tpu as pltpu
from jax.sharding import PartitionSpec as P

AB_DEV = 16
N_CHUNK = 4


def _slot_order(ab_ids, live_mask, ab_count):
    n = ab_ids.shape[0]
    key = jnp.where(live_mask, ab_ids, ab_count)
    idx = jnp.arange(n, dtype=jnp.int32)
    earlier = (key[None, :] < key[:, None]) | ((key[None, :] == key[:, None]) & (idx[None, :] < idx[:, None]))
    rank = jnp.sum(earlier.astype(jnp.int32), axis=1)
    order = jnp.sum(jnp.where(rank[None, :] == idx[:, None], idx[None, :], 0), axis=1).astype(jnp.int32)
    bounds = jnp.arange(ab_count + 1, dtype=jnp.int32)
    starts = jnp.sum((key[None, :] < bounds[:, None]).astype(jnp.int32), axis=1).astype(jnp.int32)
    return order, starts


def _ladder_kernel(order_ref, starts_ref, ab_ref, cd_ref, amp_ref, tiles_ref, out_ref, weight_ref):
    step = pl.program_id(0)
    tile = tiles_ref.shape[-1]
    groups, part, width = amp_ref.shape
    per_step = out_ref.shape[-1] // tile
    weight_ref[...] = jnp.zeros(weight_ref.shape, weight_ref.dtype)
    first = step * per_step

    def place(t, carry):
        i = order_ref[t]
        row = pl.multiple_of(cd_ref[i] * tile, tile)
        col = pl.multiple_of((ab_ref[i] - first) * tile, tile)
        weight_ref[pl.ds(row, tile), pl.ds(col, tile)] = tiles_ref[i]
        return carry

    lax.fori_loop(starts_ref[first], starts_ref[first + per_step], place, 0)
    lhs = amp_ref[...].reshape(groups * part, width)
    out_ref[...] = jnp.dot(lhs, weight_ref[...], preferred_element_type=jnp.float32)


def _ladder_products(amp3, tiles, order, starts, ab_ids, cd_ids, ab_count):
    groups, part, width = amp3.shape
    rows = groups * part
    n, tile, _ = tiles.shape
    per_step = 4 if ab_count % 8 == 0 else 1
    steps_per_half = ab_count // (2 * per_step)
    cost = pl.CostEstimate(
        flops=2 * rows * width * ab_count * tile,
        transcendentals=0,
        bytes_accessed=rows * width * 2 + tiles.size * 2 + rows * ab_count * tile * 4,
    )
    grid_spec = pltpu.PrefetchScalarGridSpec(
        num_scalar_prefetch=4,
        grid=(ab_count // per_step,),
        in_specs=[
            pl.BlockSpec((groups, part, width), lambda j, *_: (0, 0, 0)),
            pl.BlockSpec((n, tile, tile), lambda j, *_: (0, 0, 0)),
        ],
        out_specs=pl.BlockSpec(
            (None, rows, per_step * tile), lambda j, *_: (j // steps_per_half, 0, j % steps_per_half)
        ),
        scratch_shapes=[pltpu.VMEM((width, per_step * tile), tiles.dtype)],
    )
    return pl.pallas_call(
        _ladder_kernel,
        grid_spec=grid_spec,
        out_shape=jax.ShapeDtypeStruct((2, rows, ab_count * tile // 2), jnp.float32),
        cost_estimate=cost,
    )(order, starts, ab_ids, cd_ids, amp3, tiles)


class _Halving:
    def __init__(self, partial, bit_order, rep_count):
        self.levels = rep_count.bit_length() - 1
        self.part = partial.shape[0] // rep_count
        self.width = partial.shape[-1]
        self.x = partial.reshape((2,) * self.levels + (self.part, self.width))
        self.axis_bits = list(range(self.levels - 1, -1, -1))
        self.todo = list(bit_order)
        self.rep_count = rep_count

    def advance(self, rep_index):
        if not self.todo:
            return
        bit = self.todo.pop(0)
        ax = self.axis_bits.index(bit)
        mine = (rep_index >> bit) & 1
        keep = lax.dynamic_index_in_dim(self.x, mine, ax, keepdims=False)
        send = lax.dynamic_index_in_dim(self.x, 1 - mine, ax, keepdims=False)
        pairs = [(i, i ^ (1 << bit)) for i in range(self.rep_count)]
        self.x = keep + lax.ppermute(send, "rep", perm=pairs)
        self.axis_bits.pop(ax)

    def result(self):
        return self.x.reshape(self.part, self.width)


def on_device(amplitudes, integrals, ab_list, cd_list, live_count):
    own_count = lax.axis_size("own")
    rep_count = lax.axis_size("rep")
    peer_count = own_count * rep_count
    slot_count = integrals.shape[0] // peer_count
    received = lax.all_to_all(integrals, ("own", "rep"), split_axis=0, concat_axis=0, tiled=True)
    ab_ids = ab_list.reshape(-1)
    cd_ids = cd_list.reshape(-1)
    live_mask = (
        jnp.arange(slot_count, dtype=jnp.int32)[None, :] < live_count.reshape(peer_count, 1)
    ).reshape(-1)
    order, starts = _slot_order(ab_ids, live_mask, AB_DEV)
    local_rows, width = amplitudes.shape
    subs = rep_count // own_count
    part = local_rows // (subs * N_CHUNK)
    local4 = amplitudes.reshape(subs, N_CHUNK, part, width)
    rep_index = lax.axis_index("rep")
    levels = rep_count.bit_length() - 1
    orders = (list(range(levels)), [0] + list(range(levels - 1, 0, -1)))
    gathered = [lax.all_gather(local4[:, c], "own", axis=0, tiled=True) for c in range(N_CHUNK)]
    flows = []
    for chunk in range(N_CHUNK):
        for flow in flows:
            flow.advance(rep_index)
        if flows and chunk < N_CHUNK - 1:
            amp3, held = lax.optimization_barrier((gathered[chunk], [f.x for f in flows]))
            for flow, x in zip(flows, held):
                flow.x = x
        else:
            amp3 = gathered[chunk]
        partial = _ladder_products(amp3, received, order, starts, ab_ids, cd_ids, AB_DEV)
        flows.extend(_Halving(partial[h], orders[h], rep_count) for h in range(2))
    while any(flow.todo for flow in flows):
        for flow in flows:
            flow.advance(rep_index)
    pieces = [
        jnp.concatenate([flows[2 * c].result(), flows[2 * c + 1].result()], axis=1)
        for c in range(N_CHUNK)
    ]
    return jnp.concatenate(pieces, axis=0)


def solution(mesh):
    return jax.shard_map(
        on_device,
        mesh=mesh,
        in_specs=(
            P("own", "rep"),
            P(("own", "rep"), None, None),
            P(("own", "rep"), None, None),
            P(("own", "rep"), None, None),
            P(("own", "rep"), None),
        ),
        out_specs=P("rep", "own"),
        check_vma=False,
    )
```

```python
import functools

import jax
import jax.numpy as jnp
from jax import lax
from jax.experimental import pallas as pl
from jax.experimental.pallas import tpu as pltpu
from jax.sharding import PartitionSpec as P

AB_DEV = 16
N_CHUNK = 4


def _slot_order(ab_ids, live_mask, ab_count):
    n = ab_ids.shape[0]
    key = jnp.where(live_mask, ab_ids, ab_count)
    idx = jnp.arange(n, dtype=jnp.int32)
    earlier = (key[None, :] < key[:, None]) | ((key[None, :] == key[:, None]) & (idx[None, :] < idx[:, None]))
    rank = jnp.sum(earlier.astype(jnp.int32), axis=1)
    order = jnp.sum(jnp.where(rank[None, :] == idx[:, None], idx[None, :], 0), axis=1).astype(jnp.int32)
    bounds = jnp.arange(ab_count + 1, dtype=jnp.int32)
    starts = jnp.sum((key[None, :] < bounds[:, None]).astype(jnp.int32), axis=1).astype(jnp.int32)
    return order, starts


def _ladder_kernel(order_ref, starts_ref, ab_ref, cd_ref, amp_ref, tiles_ref, out_ref, weight_ref):
    step = pl.program_id(0)
    tile = tiles_ref.shape[-1]
    groups, part, width = amp_ref.shape
    per_step = out_ref.shape[-1] // tile
    weight_ref[...] = jnp.zeros(weight_ref.shape, weight_ref.dtype)
    first = step * per_step

    def place(t, carry):
        i = order_ref[t]
        row = pl.multiple_of(cd_ref[i] * tile, tile)
        col = pl.multiple_of((ab_ref[i] - first) * tile, tile)
        weight_ref[pl.ds(row, tile), pl.ds(col, tile)] = tiles_ref[i]
        return carry

    lax.fori_loop(starts_ref[first], starts_ref[first + per_step], place, 0)
    lhs = amp_ref[...].reshape(groups * part, width)
    out_ref[...] = jnp.dot(lhs, weight_ref[...], preferred_element_type=jnp.float32)


def _ladder_products(amp3, tiles, order, starts, ab_ids, cd_ids, ab_count):
    groups, part, width = amp3.shape
    rows = groups * part
    n, tile, _ = tiles.shape
    per_step = ab_count // 2 if ab_count % 2 == 0 else 1
    steps_per_half = ab_count // (2 * per_step)
    cost = pl.CostEstimate(
        flops=2 * rows * width * ab_count * tile,
        transcendentals=0,
        bytes_accessed=rows * width * 2 + tiles.size * 2 + rows * ab_count * tile * 4,
    )
    grid_spec = pltpu.PrefetchScalarGridSpec(
        num_scalar_prefetch=4,
        grid=(ab_count // per_step,),
        in_specs=[
            pl.BlockSpec((groups, part, width), lambda j, *_: (0, 0, 0)),
            pl.BlockSpec((n, tile, tile), lambda j, *_: (0, 0, 0)),
        ],
        out_specs=pl.BlockSpec(
            (None, rows, per_step * tile), lambda j, *_: (j // steps_per_half, 0, j % steps_per_half)
        ),
        scratch_shapes=[pltpu.VMEM((width, per_step * tile), tiles.dtype)],
    )
    return pl.pallas_call(
        _ladder_kernel,
        grid_spec=grid_spec,
        out_shape=jax.ShapeDtypeStruct((2, rows, ab_count * tile // 2), jnp.float32),
        cost_estimate=cost,
    )(order, starts, ab_ids, cd_ids, amp3, tiles)


class _Halving:
    def __init__(self, partial, bit_order, rep_count):
        self.levels = rep_count.bit_length() - 1
        self.part = partial.shape[0] // rep_count
        self.width = partial.shape[-1]
        self.x = partial.reshape((2,) * self.levels + (self.part, self.width))
        self.axis_bits = list(range(self.levels - 1, -1, -1))
        self.todo = list(bit_order)
        self.rep_count = rep_count

    def advance(self, rep_index):
        if not self.todo:
            return
        bit = self.todo.pop(0)
        ax = self.axis_bits.index(bit)
        mine = (rep_index >> bit) & 1
        keep = lax.dynamic_index_in_dim(self.x, mine, ax, keepdims=False)
        send = lax.dynamic_index_in_dim(self.x, 1 - mine, ax, keepdims=False)
        pairs = [(i, i ^ (1 << bit)) for i in range(self.rep_count)]
        self.x = keep + lax.ppermute(send, "rep", perm=pairs)
        self.axis_bits.pop(ax)

    def result(self):
        return self.x.reshape(self.part, self.width)


def on_device(amplitudes, integrals, ab_list, cd_list, live_count):
    own_count = lax.axis_size("own")
    rep_count = lax.axis_size("rep")
    peer_count = own_count * rep_count
    slot_count = integrals.shape[0] // peer_count
    received = lax.all_to_all(integrals, ("own", "rep"), split_axis=0, concat_axis=0, tiled=True)
    ab_ids = ab_list.reshape(-1)
    cd_ids = cd_list.reshape(-1)
    live_mask = (
        jnp.arange(slot_count, dtype=jnp.int32)[None, :] < live_count.reshape(peer_count, 1)
    ).reshape(-1)
    order, starts = _slot_order(ab_ids, live_mask, AB_DEV)
    local_rows, width = amplitudes.shape
    subs = rep_count // own_count
    part = local_rows // (subs * N_CHUNK)
    local4 = amplitudes.reshape(subs, N_CHUNK, part, width)
    rep_index = lax.axis_index("rep")
    levels = rep_count.bit_length() - 1
    orders = (list(range(levels)), [0] + list(range(levels - 1, 0, -1)))
    gathered = [lax.all_gather(local4[:, c], "own", axis=0, tiled=True) for c in range(N_CHUNK)]
    flows = []
    for chunk in range(N_CHUNK):
        for flow in flows:
            flow.advance(rep_index)
        if flows:
            amp3, held = lax.optimization_barrier((gathered[chunk], [f.x for f in flows]))
            for flow, x in zip(flows, held):
                flow.x = x
        else:
            amp3 = gathered[chunk]
        partial = _ladder_products(amp3, received, order, starts, ab_ids, cd_ids, AB_DEV)
        flows.extend(_Halving(partial[h], orders[h], rep_count) for h in range(2))
    while any(flow.todo for flow in flows):
        for flow in flows:
            flow.advance(rep_index)
    pieces = [
        jnp.concatenate([flows[2 * c].result(), flows[2 * c + 1].result()], axis=1)
        for c in range(N_CHUNK)
    ]
    return jnp.concatenate(pieces, axis=0)


def solution(mesh):
    return jax.shard_map(
        on_device,
        mesh=mesh,
        in_specs=(
            P("own", "rep"),
            P(("own", "rep"), None, None),
            P(("own", "rep"), None, None),
            P(("own", "rep"), None, None),
            P(("own", "rep"), None),
        ),
        out_specs=P("rep", "own"),
        check_vma=False,
    )
```

```python
import functools

import jax
import jax.numpy as jnp
from jax import lax
from jax.experimental import pallas as pl
from jax.experimental.pallas import tpu as pltpu
from jax.sharding import PartitionSpec as P

AB_DEV = 16
N_CHUNK = 4


def _slot_order(ab_ids, live_mask, ab_count):
    n = ab_ids.shape[0]
    key = jnp.where(live_mask, ab_ids, ab_count)
    idx = jnp.arange(n, dtype=jnp.int32)
    earlier = (key[None, :] < key[:, None]) | ((key[None, :] == key[:, None]) & (idx[None, :] < idx[:, None]))
    rank = jnp.sum(earlier.astype(jnp.int32), axis=1)
    order = jnp.sum(jnp.where(rank[None, :] == idx[:, None], idx[None, :], 0), axis=1).astype(jnp.int32)
    bounds = jnp.arange(ab_count + 1, dtype=jnp.int32)
    starts = jnp.sum((key[None, :] < bounds[:, None]).astype(jnp.int32), axis=1).astype(jnp.int32)
    return order, starts


def _ladder_kernel(order_ref, starts_ref, ab_ref, cd_ref, amp_ref, tiles_ref, out_ref, weight_ref):
    step = pl.program_id(0)
    tile = tiles_ref.shape[-1]
    groups, part, width = amp_ref.shape
    per_step = out_ref.shape[-1] // tile
    weight_ref[...] = jnp.zeros(weight_ref.shape, weight_ref.dtype)
    first = step * per_step

    def place(t, carry):
        i = order_ref[t]
        row = pl.multiple_of(cd_ref[i] * tile, tile)
        col = pl.multiple_of((ab_ref[i] - first) * tile, tile)
        weight_ref[pl.ds(row, tile), pl.ds(col, tile)] = tiles_ref[i]
        return carry

    lax.fori_loop(starts_ref[first], starts_ref[first + per_step], place, 0)
    lhs = amp_ref[...].reshape(groups * part, width)
    out_ref[...] = jnp.dot(lhs, weight_ref[...], preferred_element_type=jnp.float32)


def _ladder_products(amp3, tiles, order, starts, ab_ids, cd_ids, ab_count):
    groups, part, width = amp3.shape
    rows = groups * part
    n, tile, _ = tiles.shape
    per_step = 4 if ab_count % 8 == 0 else 1
    steps_per_half = ab_count // (2 * per_step)
    cost = pl.CostEstimate(
        flops=2 * rows * width * ab_count * tile,
        transcendentals=0,
        bytes_accessed=rows * width * 2 + tiles.size * 2 + rows * ab_count * tile * 4,
    )
    grid_spec = pltpu.PrefetchScalarGridSpec(
        num_scalar_prefetch=4,
        grid=(ab_count // per_step,),
        in_specs=[
            pl.BlockSpec((groups, part, width), lambda j, *_: (0, 0, 0)),
            pl.BlockSpec((n, tile, tile), lambda j, *_: (0, 0, 0)),
        ],
        out_specs=pl.BlockSpec(
            (None, rows, per_step * tile), lambda j, *_: (j // steps_per_half, 0, j % steps_per_half)
        ),
        scratch_shapes=[pltpu.VMEM((width, per_step * tile), tiles.dtype)],
    )
    return pl.pallas_call(
        _ladder_kernel,
        grid_spec=grid_spec,
        out_shape=jax.ShapeDtypeStruct((2, rows, ab_count * tile // 2), jnp.float32),
        cost_estimate=cost,
    )(order, starts, ab_ids, cd_ids, amp3, tiles)


class _Halving:
    def __init__(self, partial, bit_order, rep_count):
        self.levels = rep_count.bit_length() - 1
        self.part = partial.shape[0] // rep_count
        self.width = partial.shape[-1]
        self.x = partial.reshape((2,) * self.levels + (self.part, self.width))
        self.axis_bits = list(range(self.levels - 1, -1, -1))
        self.todo = list(bit_order)
        self.rep_count = rep_count

    def advance(self, rep_index):
        if not self.todo:
            return
        bit = self.todo.pop(0)
        ax = self.axis_bits.index(bit)
        mine = (rep_index >> bit) & 1
        keep = lax.dynamic_index_in_dim(self.x, mine, ax, keepdims=False)
        send = lax.dynamic_index_in_dim(self.x, 1 - mine, ax, keepdims=False)
        pairs = [(i, i ^ (1 << bit)) for i in range(self.rep_count)]
        self.x = keep + lax.ppermute(send, "rep", perm=pairs)
        self.axis_bits.pop(ax)

    def result(self):
        return self.x.reshape(self.part, self.width)


def on_device(amplitudes, integrals, ab_list, cd_list, live_count):
    own_count = lax.axis_size("own")
    rep_count = lax.axis_size("rep")
    peer_count = own_count * rep_count
    slot_count = integrals.shape[0] // peer_count

    ab_ids = ab_list.reshape(-1)
    cd_ids = cd_list.reshape(-1)
    live_mask = (
        jnp.arange(slot_count, dtype=jnp.int32)[None, :] < live_count.reshape(peer_count, 1)
    ).reshape(-1)
    order, starts = _slot_order(ab_ids, live_mask, AB_DEV)
    local_rows, width = amplitudes.shape
    subs = rep_count // own_count
    part = local_rows // (subs * N_CHUNK)
    local4 = amplitudes.reshape(subs, N_CHUNK, part, width)
    rep_index = lax.axis_index("rep")
    levels = rep_count.bit_length() - 1
    orders = (list(range(levels)), [0] + list(range(levels - 1, 0, -1)))
    gathered = [lax.all_gather(local4[:, c], "own", axis=0, tiled=True) for c in range(N_CHUNK)]
    _, integrals_in = lax.optimization_barrier((gathered[0], integrals))
    received = lax.all_to_all(integrals_in, ("own", "rep"), split_axis=0, concat_axis=0, tiled=True)
    flows = []
    for chunk in range(N_CHUNK):
        for flow in flows:
            flow.advance(rep_index)
        if flows:
            amp3, held = lax.optimization_barrier((gathered[chunk], [f.x for f in flows]))
            for flow, x in zip(flows, held):
                flow.x = x
        else:
            amp3 = gathered[chunk]
        partial = _ladder_products(amp3, received, order, starts, ab_ids, cd_ids, AB_DEV)
        flows.extend(_Halving(partial[h], orders[h], rep_count) for h in range(2))
    while any(flow.todo for flow in flows):
        for flow in flows:
            flow.advance(rep_index)
    pieces = [
        jnp.concatenate([flows[2 * c].result(), flows[2 * c + 1].result()], axis=1)
        for c in range(N_CHUNK)
    ]
    return jnp.concatenate(pieces, axis=0)


def solution(mesh):
    return jax.shard_map(
        on_device,
        mesh=mesh,
        in_specs=(
            P("own", "rep"),
            P(("own", "rep"), None, None),
            P(("own", "rep"), None, None),
            P(("own", "rep"), None, None),
            P(("own", "rep"), None),
        ),
        out_specs=P("rep", "own"),
        check_vma=False,
    )
```

```python
import functools

import jax
import jax.numpy as jnp
from jax import lax
from jax.experimental import pallas as pl
from jax.experimental.pallas import tpu as pltpu
from jax.sharding import PartitionSpec as P

AB_DEV = 16
N_CHUNK = 4


def _slot_order(ab_ids, live_mask, ab_count):
    n = ab_ids.shape[0]
    key = jnp.where(live_mask, ab_ids, ab_count)
    idx = jnp.arange(n, dtype=jnp.int32)
    earlier = (key[None, :] < key[:, None]) | ((key[None, :] == key[:, None]) & (idx[None, :] < idx[:, None]))
    rank = jnp.sum(earlier.astype(jnp.int32), axis=1)
    order = jnp.sum(jnp.where(rank[None, :] == idx[:, None], idx[None, :], 0), axis=1).astype(jnp.int32)
    bounds = jnp.arange(ab_count + 1, dtype=jnp.int32)
    starts = jnp.sum((key[None, :] < bounds[:, None]).astype(jnp.int32), axis=1).astype(jnp.int32)
    return order, starts


def _ladder_kernel(order_ref, starts_ref, ab_ref, cd_ref, amp_ref, tiles_ref, out_ref, weight_ref):
    step = pl.program_id(0)
    tile = tiles_ref.shape[-1]
    groups, part, width = amp_ref.shape
    per_step = out_ref.shape[-1] // tile
    weight_ref[...] = jnp.zeros(weight_ref.shape, weight_ref.dtype)
    first = step * per_step

    def place(t, carry):
        i = order_ref[t]
        row = pl.multiple_of(cd_ref[i] * tile, tile)
        col = pl.multiple_of((ab_ref[i] - first) * tile, tile)
        weight_ref[pl.ds(row, tile), pl.ds(col, tile)] = tiles_ref[i]
        return carry

    lax.fori_loop(starts_ref[first], starts_ref[first + per_step], place, 0)
    lhs = amp_ref[...].reshape(groups * part, width)
    out_ref[...] = jnp.dot(lhs, weight_ref[...], preferred_element_type=jnp.float32)


def _ladder_products(amp3, tiles, order, starts, ab_ids, cd_ids, ab_count):
    groups, part, width = amp3.shape
    rows = groups * part
    n, tile, _ = tiles.shape
    per_step = 4 if ab_count % 8 == 0 else 1
    steps_per_half = ab_count // (2 * per_step)
    cost = pl.CostEstimate(
        flops=2 * rows * width * ab_count * tile,
        transcendentals=0,
        bytes_accessed=rows * width * 2 + tiles.size * 2 + rows * ab_count * tile * 4,
    )
    grid_spec = pltpu.PrefetchScalarGridSpec(
        num_scalar_prefetch=4,
        grid=(ab_count // per_step,),
        in_specs=[
            pl.BlockSpec((groups, part, width), lambda j, *_: (0, 0, 0)),
            pl.BlockSpec((n, tile, tile), lambda j, *_: (0, 0, 0)),
        ],
        out_specs=pl.BlockSpec(
            (None, rows, per_step * tile), lambda j, *_: (j // steps_per_half, 0, j % steps_per_half)
        ),
        scratch_shapes=[pltpu.VMEM((width, per_step * tile), tiles.dtype)],
    )
    return pl.pallas_call(
        _ladder_kernel,
        grid_spec=grid_spec,
        out_shape=jax.ShapeDtypeStruct((2, rows, ab_count * tile // 2), jnp.float32),
        cost_estimate=cost,
    )(order, starts, ab_ids, cd_ids, amp3, tiles)


class _Halving:
    def __init__(self, partial, bit_order, rep_count):
        self.levels = rep_count.bit_length() - 1
        self.part = partial.shape[0] // rep_count
        self.width = partial.shape[-1]
        self.x = partial.reshape((2,) * self.levels + (self.part, self.width))
        self.axis_bits = list(range(self.levels - 1, -1, -1))
        self.todo = list(bit_order)
        self.rep_count = rep_count

    def advance(self, rep_index):
        if not self.todo:
            return
        bit = self.todo.pop(0)
        ax = self.axis_bits.index(bit)
        mine = (rep_index >> bit) & 1
        keep = lax.dynamic_index_in_dim(self.x, mine, ax, keepdims=False)
        send = lax.dynamic_index_in_dim(self.x, 1 - mine, ax, keepdims=False)
        pairs = [(i, i ^ (1 << bit)) for i in range(self.rep_count)]
        self.x = keep + lax.ppermute(send, "rep", perm=pairs)
        self.axis_bits.pop(ax)

    def result(self):
        return self.x.reshape(self.part, self.width)


class _Pair:
    def __init__(self, partial2, orders, rep_count):
        self.levels = rep_count.bit_length() - 1
        self.rep_count = rep_count
        self.part = partial2.shape[1] // rep_count
        self.width = partial2.shape[2]
        self.joint = partial2.reshape((2,) + (2,) * self.levels + (self.part, self.width))
        self.orders = orders
        self.halves = None

    @property
    def todo(self):
        return self.halves is None or any(h.todo for h in self.halves)

    @property
    def x(self):
        return self.joint if self.halves is None else [h.x for h in self.halves]

    @x.setter
    def x(self, value):
        if self.halves is None:
            self.joint = value
        else:
            for h, v in zip(self.halves, value):
                h.x = v

    def advance(self, rep_index):
        if self.halves is not None:
            for h in self.halves:
                h.advance(rep_index)
            return
        bit = self.orders[0][0]
        ax = 1 + (self.levels - 1 - bit)
        mine = (rep_index >> bit) & 1
        keep = lax.dynamic_index_in_dim(self.joint, mine, ax, keepdims=False)
        send = lax.dynamic_index_in_dim(self.joint, 1 - mine, ax, keepdims=False)
        pairs = [(i, i ^ (1 << bit)) for i in range(self.rep_count)]
        both = keep + lax.ppermute(send, "rep", perm=pairs)
        self.halves = []
        for h in range(2):
            flow = object.__new__(_Halving)
            flow.levels, flow.part, flow.width = self.levels, self.part, self.width
            flow.rep_count = self.rep_count
            flow.x = both[h]
            flow.axis_bits = [b for b in range(self.levels - 1, -1, -1) if b != bit]
            flow.todo = list(self.orders[h][1:])
            self.halves.append(flow)

    def result(self):
        return jnp.concatenate([h.result() for h in self.halves], axis=1)


def on_device(amplitudes, integrals, ab_list, cd_list, live_count):
    own_count = lax.axis_size("own")
    rep_count = lax.axis_size("rep")
    peer_count = own_count * rep_count
    slot_count = integrals.shape[0] // peer_count
    received = lax.all_to_all(integrals, ("own", "rep"), split_axis=0, concat_axis=0, tiled=True)
    ab_ids = ab_list.reshape(-1)
    cd_ids = cd_list.reshape(-1)
    live_mask = (
        jnp.arange(slot_count, dtype=jnp.int32)[None, :] < live_count.reshape(peer_count, 1)
    ).reshape(-1)
    order, starts = _slot_order(ab_ids, live_mask, AB_DEV)
    local_rows, width = amplitudes.shape
    subs = rep_count // own_count
    part = local_rows // (subs * N_CHUNK)
    local4 = amplitudes.reshape(subs, N_CHUNK, part, width)
    rep_index = lax.axis_index("rep")
    levels = rep_count.bit_length() - 1
    orders = (list(range(levels)), [0] + list(range(levels - 1, 0, -1)))
    gathered = [lax.all_gather(local4[:, c], "own", axis=0, tiled=True) for c in range(N_CHUNK)]
    flows = []
    for chunk in range(N_CHUNK):
        for flow in flows:
            flow.advance(rep_index)
        if flows:
            amp3, held = lax.optimization_barrier((gathered[chunk], [f.x for f in flows]))
            for flow, x in zip(flows, held):
                flow.x = x
        else:
            amp3 = gathered[chunk]
        partial = _ladder_products(amp3, received, order, starts, ab_ids, cd_ids, AB_DEV)
        flows.append(_Pair(partial, orders, rep_count))
    while any(flow.todo for flow in flows):
        for flow in flows:
            flow.advance(rep_index)
    pieces = [flow.result() for flow in flows]
    return jnp.concatenate(pieces, axis=0)


def solution(mesh):
    return jax.shard_map(
        on_device,
        mesh=mesh,
        in_specs=(
            P("own", "rep"),
            P(("own", "rep"), None, None),
            P(("own", "rep"), None, None),
            P(("own", "rep"), None, None),
            P(("own", "rep"), None),
        ),
        out_specs=P("rep", "own"),
        check_vma=False,
    )
```

```python
import functools

import jax
import jax.numpy as jnp
from jax import lax
from jax.experimental import pallas as pl
from jax.experimental.pallas import tpu as pltpu
from jax.sharding import PartitionSpec as P

AB_DEV = 16
N_CHUNK = 4


def _slot_order(ab_ids, live_mask, ab_count):
    n = ab_ids.shape[0]
    key = jnp.where(live_mask, ab_ids, ab_count)
    idx = jnp.arange(n, dtype=jnp.int32)
    earlier = (key[None, :] < key[:, None]) | ((key[None, :] == key[:, None]) & (idx[None, :] < idx[:, None]))
    rank = jnp.sum(earlier.astype(jnp.int32), axis=1)
    order = jnp.sum(jnp.where(rank[None, :] == idx[:, None], idx[None, :], 0), axis=1).astype(jnp.int32)
    bounds = jnp.arange(ab_count + 1, dtype=jnp.int32)
    starts = jnp.sum((key[None, :] < bounds[:, None]).astype(jnp.int32), axis=1).astype(jnp.int32)
    return order, starts


def _ladder_kernel(order_ref, starts_ref, ab_ref, cd_ref, amp_ref, tiles_ref, out_ref, weight_ref):
    step = pl.program_id(0)
    tile = tiles_ref.shape[-1]
    groups, part, width = amp_ref.shape
    per_step = out_ref.shape[-1] // tile
    weight_ref[...] = jnp.zeros(weight_ref.shape, weight_ref.dtype)
    first = step * per_step

    def place(t, carry):
        i = order_ref[t]
        row = pl.multiple_of(cd_ref[i] * tile, tile)
        col = pl.multiple_of((ab_ref[i] - first) * tile, tile)
        weight_ref[pl.ds(row, tile), pl.ds(col, tile)] = tiles_ref[i]
        return carry

    lax.fori_loop(starts_ref[first], starts_ref[first + per_step], place, 0)
    lhs = amp_ref[...].reshape(groups * part, width)
    out_ref[...] = jnp.dot(lhs, weight_ref[...], preferred_element_type=jnp.float32)


def _ladder_products(amp3, tiles, order, starts, ab_ids, cd_ids, ab_count):
    groups, part, width = amp3.shape
    rows = groups * part
    n, tile, _ = tiles.shape
    per_step = ab_count // 2 if ab_count % 2 == 0 else 1
    steps_per_half = ab_count // (2 * per_step)
    cost = pl.CostEstimate(
        flops=2 * rows * width * ab_count * tile,
        transcendentals=0,
        bytes_accessed=rows * width * 2 + tiles.size * 2 + rows * ab_count * tile * 4,
    )
    grid_spec = pltpu.PrefetchScalarGridSpec(
        num_scalar_prefetch=4,
        grid=(ab_count // per_step,),
        in_specs=[
            pl.BlockSpec((groups, part, width), lambda j, *_: (0, 0, 0)),
            pl.BlockSpec((n, tile, tile), lambda j, *_: (0, 0, 0)),
        ],
        out_specs=pl.BlockSpec(
            (None, rows, per_step * tile), lambda j, *_: (j // steps_per_half, 0, j % steps_per_half)
        ),
        scratch_shapes=[pltpu.VMEM((width, per_step * tile), tiles.dtype)],
    )
    return pl.pallas_call(
        _ladder_kernel,
        grid_spec=grid_spec,
        out_shape=jax.ShapeDtypeStruct((2, rows, ab_count * tile // 2), jnp.float32),
        cost_estimate=cost,
    )(order, starts, ab_ids, cd_ids, amp3, tiles)


class _Halving:
    def __init__(self, partial, bit_order, rep_count):
        self.levels = rep_count.bit_length() - 1
        self.part = partial.shape[0] // rep_count
        self.width = partial.shape[-1]
        self.x = partial.reshape((2,) * self.levels + (self.part, self.width))
        self.axis_bits = list(range(self.levels - 1, -1, -1))
        self.todo = list(bit_order)
        self.rep_count = rep_count

    def advance(self, rep_index):
        if not self.todo:
            return
        bit = self.todo.pop(0)
        ax = self.axis_bits.index(bit)
        mine = (rep_index >> bit) & 1
        keep = lax.dynamic_index_in_dim(self.x, mine, ax, keepdims=False)
        send = lax.dynamic_index_in_dim(self.x, 1 - mine, ax, keepdims=False)
        pairs = [(i, i ^ (1 << bit)) for i in range(self.rep_count)]
        self.x = keep + lax.ppermute(send, "rep", perm=pairs)
        self.axis_bits.pop(ax)

    def result(self):
        return self.x.reshape(self.part, self.width)


class _Pair:
    def __init__(self, partial2, orders, rep_count):
        self.levels = rep_count.bit_length() - 1
        self.rep_count = rep_count
        self.part = partial2.shape[1] // rep_count
        self.width = partial2.shape[2]
        self.joint = partial2.reshape((2,) + (2,) * self.levels + (self.part, self.width))
        self.orders = orders
        self.halves = None

    @property
    def todo(self):
        return self.halves is None or any(h.todo for h in self.halves)

    @property
    def x(self):
        return self.joint if self.halves is None else [h.x for h in self.halves]

    @x.setter
    def x(self, value):
        if self.halves is None:
            self.joint = value
        else:
            for h, v in zip(self.halves, value):
                h.x = v

    def advance(self, rep_index):
        if self.halves is not None:
            for h in self.halves:
                h.advance(rep_index)
            return
        bit = self.orders[0][0]
        ax = 1 + (self.levels - 1 - bit)
        mine = (rep_index >> bit) & 1
        keep = lax.dynamic_index_in_dim(self.joint, mine, ax, keepdims=False)
        send = lax.dynamic_index_in_dim(self.joint, 1 - mine, ax, keepdims=False)
        pairs = [(i, i ^ (1 << bit)) for i in range(self.rep_count)]
        both = keep + lax.ppermute(send, "rep", perm=pairs)
        self.halves = []
        for h in range(2):
            flow = object.__new__(_Halving)
            flow.levels, flow.part, flow.width = self.levels, self.part, self.width
            flow.rep_count = self.rep_count
            flow.x = both[h]
            flow.axis_bits = [b for b in range(self.levels - 1, -1, -1) if b != bit]
            flow.todo = list(self.orders[h][1:])
            self.halves.append(flow)

    def result(self):
        return jnp.concatenate([h.result() for h in self.halves], axis=1)


def on_device(amplitudes, integrals, ab_list, cd_list, live_count):
    own_count = lax.axis_size("own")
    rep_count = lax.axis_size("rep")
    peer_count = own_count * rep_count
    slot_count = integrals.shape[0] // peer_count
    received = lax.all_to_all(integrals, ("own", "rep"), split_axis=0, concat_axis=0, tiled=True)
    ab_ids = ab_list.reshape(-1)
    cd_ids = cd_list.reshape(-1)
    live_mask = (
        jnp.arange(slot_count, dtype=jnp.int32)[None, :] < live_count.reshape(peer_count, 1)
    ).reshape(-1)
    order, starts = _slot_order(ab_ids, live_mask, AB_DEV)
    local_rows, width = amplitudes.shape
    subs = rep_count // own_count
    part = local_rows // (subs * N_CHUNK)
    local4 = amplitudes.reshape(subs, N_CHUNK, part, width)
    rep_index = lax.axis_index("rep")
    levels = rep_count.bit_length() - 1
    orders = (list(range(levels)), [0] + list(range(levels - 1, 0, -1)))
    gathered = [lax.all_gather(local4[:, c], "own", axis=0, tiled=True) for c in range(N_CHUNK)]
    flows = []
    for chunk in range(N_CHUNK):
        for flow in flows:
            flow.advance(rep_index)
        if flows:
            amp3, held = lax.optimization_barrier((gathered[chunk], [f.x for f in flows]))
            for flow, x in zip(flows, held):
                flow.x = x
        else:
            amp3 = gathered[chunk]
        partial = _ladder_products(amp3, received, order, starts, ab_ids, cd_ids, AB_DEV)
        flows.append(_Pair(partial, orders, rep_count))
    while any(flow.todo for flow in flows):
        for flow in flows:
            flow.advance(rep_index)
    pieces = [flow.result() for flow in flows]
    return jnp.concatenate(pieces, axis=0)


def solution(mesh):
    return jax.shard_map(
        on_device,
        mesh=mesh,
        in_specs=(
            P("own", "rep"),
            P(("own", "rep"), None, None),
            P(("own", "rep"), None, None),
            P(("own", "rep"), None, None),
            P(("own", "rep"), None),
        ),
        out_specs=P("rep", "own"),
        check_vma=False,
    )
```

```python
import functools

import jax
import jax.numpy as jnp
from jax import lax
from jax.experimental import pallas as pl
from jax.experimental.pallas import tpu as pltpu
from jax.sharding import PartitionSpec as P

AB_DEV = 16
N_CHUNK = 4


def _slot_order(ab_ids, live_mask, ab_count):
    n = ab_ids.shape[0]
    key = jnp.where(live_mask, ab_ids, ab_count)
    idx = jnp.arange(n, dtype=jnp.int32)
    earlier = (key[None, :] < key[:, None]) | ((key[None, :] == key[:, None]) & (idx[None, :] < idx[:, None]))
    rank = jnp.sum(earlier.astype(jnp.int32), axis=1)
    order = jnp.sum(jnp.where(rank[None, :] == idx[:, None], idx[None, :], 0), axis=1).astype(jnp.int32)
    bounds = jnp.arange(ab_count + 1, dtype=jnp.int32)
    starts = jnp.sum((key[None, :] < bounds[:, None]).astype(jnp.int32), axis=1).astype(jnp.int32)
    return order, starts


def _ladder_kernel(order_ref, starts_ref, ab_ref, cd_ref, amp_ref, tiles_ref, out_ref, weight_ref):
    step = pl.program_id(0)
    tile = tiles_ref.shape[-1]
    groups, part, width = amp_ref.shape
    per_step = out_ref.shape[-1] // tile
    weight_ref[...] = jnp.zeros(weight_ref.shape, weight_ref.dtype)
    first = step * per_step

    def place(t, carry):
        i = order_ref[t]
        row = pl.multiple_of(cd_ref[i] * tile, tile)
        col = pl.multiple_of((ab_ref[i] - first) * tile, tile)
        weight_ref[pl.ds(row, tile), pl.ds(col, tile)] = tiles_ref[i]
        return carry

    lax.fori_loop(starts_ref[first], starts_ref[first + per_step], place, 0)
    lhs = amp_ref[...].reshape(groups * part, width)
    out_ref[...] = jnp.dot(lhs, weight_ref[...], preferred_element_type=jnp.float32)


def _ladder_products(amp3, tiles, order, starts, ab_ids, cd_ids, ab_count):
    groups, part, width = amp3.shape
    rows = groups * part
    n, tile, _ = tiles.shape
    per_step = ab_count // 2 if ab_count % 2 == 0 else 1
    steps_per_half = ab_count // (2 * per_step)
    cost = pl.CostEstimate(
        flops=2 * rows * tile * tile * n,
        transcendentals=0,
        bytes_accessed=rows * width * 2 + tiles.size * 2 + rows * ab_count * tile * 4,
    )
    grid_spec = pltpu.PrefetchScalarGridSpec(
        num_scalar_prefetch=4,
        grid=(ab_count // per_step,),
        in_specs=[
            pl.BlockSpec((groups, part, width), lambda j, *_: (0, 0, 0)),
            pl.BlockSpec((n, tile, tile), lambda j, *_: (0, 0, 0)),
        ],
        out_specs=pl.BlockSpec(
            (None, rows, per_step * tile), lambda j, *_: (j // steps_per_half, 0, j % steps_per_half)
        ),
        scratch_shapes=[pltpu.VMEM((width, per_step * tile), tiles.dtype)],
    )
    return pl.pallas_call(
        _ladder_kernel,
        grid_spec=grid_spec,
        out_shape=jax.ShapeDtypeStruct((2, rows, ab_count * tile // 2), jnp.float32),
        cost_estimate=cost,
    )(order, starts, ab_ids, cd_ids, amp3, tiles)


class _Halving:
    def __init__(self, partial, bit_order, rep_count):
        self.levels = rep_count.bit_length() - 1
        self.part = partial.shape[0] // rep_count
        self.width = partial.shape[-1]
        self.x = partial.reshape((2,) * self.levels + (self.part, self.width))
        self.axis_bits = list(range(self.levels - 1, -1, -1))
        self.todo = list(bit_order)
        self.rep_count = rep_count

    def advance(self, rep_index):
        if not self.todo:
            return
        bit = self.todo.pop(0)
        ax = self.axis_bits.index(bit)
        mine = (rep_index >> bit) & 1
        keep = lax.dynamic_index_in_dim(self.x, mine, ax, keepdims=False)
        send = lax.dynamic_index_in_dim(self.x, 1 - mine, ax, keepdims=False)
        pairs = [(i, i ^ (1 << bit)) for i in range(self.rep_count)]
        self.x = keep + lax.ppermute(send, "rep", perm=pairs)
        self.axis_bits.pop(ax)

    def result(self):
        return self.x.reshape(self.part, self.width)


class _Pair:
    def __init__(self, partial2, orders, rep_count):
        self.levels = rep_count.bit_length() - 1
        self.rep_count = rep_count
        self.part = partial2.shape[1] // rep_count
        self.width = partial2.shape[2]
        self.joint = partial2.reshape((2,) + (2,) * self.levels + (self.part, self.width))
        self.orders = orders
        self.halves = None

    @property
    def todo(self):
        return self.halves is None or any(h.todo for h in self.halves)

    @property
    def x(self):
        return self.joint if self.halves is None else [h.x for h in self.halves]

    @x.setter
    def x(self, value):
        if self.halves is None:
            self.joint = value
        else:
            for h, v in zip(self.halves, value):
                h.x = v

    def advance(self, rep_index):
        if self.halves is not None:
            for h in self.halves:
                h.advance(rep_index)
            return
        bit = self.orders[0][0]
        ax = 1 + (self.levels - 1 - bit)
        mine = (rep_index >> bit) & 1
        keep = lax.dynamic_index_in_dim(self.joint, mine, ax, keepdims=False)
        send = lax.dynamic_index_in_dim(self.joint, 1 - mine, ax, keepdims=False)
        pairs = [(i, i ^ (1 << bit)) for i in range(self.rep_count)]
        both = keep + lax.ppermute(send, "rep", perm=pairs)
        self.halves = []
        for h in range(2):
            flow = object.__new__(_Halving)
            flow.levels, flow.part, flow.width = self.levels, self.part, self.width
            flow.rep_count = self.rep_count
            flow.x = both[h]
            flow.axis_bits = [b for b in range(self.levels - 1, -1, -1) if b != bit]
            flow.todo = list(self.orders[h][1:])
            self.halves.append(flow)

    def result(self):
        return jnp.concatenate([h.result() for h in self.halves], axis=1)


def on_device(amplitudes, integrals, ab_list, cd_list, live_count):
    own_count = lax.axis_size("own")
    rep_count = lax.axis_size("rep")
    peer_count = own_count * rep_count
    slot_count = integrals.shape[0] // peer_count
    received = lax.all_to_all(integrals, ("own", "rep"), split_axis=0, concat_axis=0, tiled=True)
    ab_ids = ab_list.reshape(-1)
    cd_ids = cd_list.reshape(-1)
    live_mask = (
        jnp.arange(slot_count, dtype=jnp.int32)[None, :] < live_count.reshape(peer_count, 1)
    ).reshape(-1)
    order, starts = _slot_order(ab_ids, live_mask, AB_DEV)
    local_rows, width = amplitudes.shape
    subs = rep_count // own_count
    part = local_rows // (subs * N_CHUNK)
    local4 = amplitudes.reshape(subs, N_CHUNK, part, width)
    rep_index = lax.axis_index("rep")
    levels = rep_count.bit_length() - 1
    orders = (list(range(levels)), [0] + list(range(levels - 1, 0, -1)))
    gathered = [lax.all_gather(local4[:, c], "own", axis=0, tiled=True) for c in range(N_CHUNK)]
    flows = []
    for chunk in range(N_CHUNK):
        for flow in flows:
            flow.advance(rep_index)
        if flows:
            amp3, held = lax.optimization_barrier((gathered[chunk], [f.x for f in flows]))
            for flow, x in zip(flows, held):
                flow.x = x
        else:
            amp3 = gathered[chunk]
        partial = _ladder_products(amp3, received, order, starts, ab_ids, cd_ids, AB_DEV)
        flows.append(_Pair(partial, orders, rep_count))
    while any(flow.todo for flow in flows):
        for flow in flows:
            flow.advance(rep_index)
    pieces = [flow.result() for flow in flows]
    return jnp.concatenate(pieces, axis=0)


def solution(mesh):
    return jax.shard_map(
        on_device,
        mesh=mesh,
        in_specs=(
            P("own", "rep"),
            P(("own", "rep"), None, None),
            P(("own", "rep"), None, None),
            P(("own", "rep"), None, None),
            P(("own", "rep"), None),
        ),
        out_specs=P("rep", "own"),
        check_vma=False,
    )
```

```python
import functools

import jax
import jax.numpy as jnp
from jax import lax
from jax.experimental import pallas as pl
from jax.experimental.pallas import tpu as pltpu
from jax.sharding import PartitionSpec as P

AB_DEV = 16
N_CHUNK = 4


def _slot_order(ab_ids, live_mask, ab_count):
    n = ab_ids.shape[0]
    key = jnp.where(live_mask, ab_ids, ab_count)
    idx = jnp.arange(n, dtype=jnp.int32)
    earlier = (key[None, :] < key[:, None]) | ((key[None, :] == key[:, None]) & (idx[None, :] < idx[:, None]))
    rank = jnp.sum(earlier.astype(jnp.int32), axis=1)
    order = jnp.sum(jnp.where(rank[None, :] == idx[:, None], idx[None, :], 0), axis=1).astype(jnp.int32)
    bounds = jnp.arange(ab_count + 1, dtype=jnp.int32)
    starts = jnp.sum((key[None, :] < bounds[:, None]).astype(jnp.int32), axis=1).astype(jnp.int32)
    return order, starts


def _ladder_kernel(order_ref, starts_ref, ab_ref, cd_ref, amp_ref, tiles_ref, out_ref, weight_ref):
    step = pl.program_id(0)
    tile = tiles_ref.shape[-1]
    groups, part, width = amp_ref.shape
    per_step = out_ref.shape[-1] // tile
    weight_ref[...] = jnp.zeros(weight_ref.shape, weight_ref.dtype)
    first = step * per_step

    def place(t, carry):
        i = order_ref[t]
        row = pl.multiple_of(cd_ref[i] * tile, tile)
        col = pl.multiple_of((ab_ref[i] - first) * tile, tile)
        weight_ref[pl.ds(row, tile), pl.ds(col, tile)] = tiles_ref[i]
        return carry

    lax.fori_loop(starts_ref[first], starts_ref[first + per_step], place, 0)
    lhs = amp_ref[...].reshape(groups * part, width)
    out_ref[...] = jnp.dot(lhs, weight_ref[...], preferred_element_type=jnp.float32)


def _ladder_products(amp3, tiles, order, starts, ab_ids, cd_ids, ab_count):
    groups, part, width = amp3.shape
    rows = groups * part
    n, tile, _ = tiles.shape
    per_step = ab_count // 2 if ab_count % 2 == 0 else 1
    steps_per_half = ab_count // (2 * per_step)
    cost = pl.CostEstimate(
        flops=2 * rows * width * ab_count * tile,
        transcendentals=0,
        bytes_accessed=rows * width * 2 + tiles.size * 2 + rows * ab_count * tile * 4,
    )
    grid_spec = pltpu.PrefetchScalarGridSpec(
        num_scalar_prefetch=4,
        grid=(ab_count // per_step,),
        in_specs=[
            pl.BlockSpec((groups, part, width), lambda j, *_: (0, 0, 0)),
            pl.BlockSpec((n, tile, tile), lambda j, *_: (0, 0, 0)),
        ],
        out_specs=pl.BlockSpec(
            (None, rows, per_step * tile), lambda j, *_: (j // steps_per_half, 0, j % steps_per_half)
        ),
        scratch_shapes=[pltpu.VMEM((width, per_step * tile), tiles.dtype)],
    )
    return pl.pallas_call(
        _ladder_kernel,
        grid_spec=grid_spec,
        out_shape=jax.ShapeDtypeStruct((2, rows, ab_count * tile // 2), jnp.float32),
        cost_estimate=cost,
    )(order, starts, ab_ids, cd_ids, amp3, tiles)


class _Halving:
    def __init__(self, partial, bit_order, rep_count):
        self.levels = rep_count.bit_length() - 1
        self.part = partial.shape[0] // rep_count
        self.width = partial.shape[-1]
        self.x = partial.reshape((2,) * self.levels + (self.part, self.width))
        self.axis_bits = list(range(self.levels - 1, -1, -1))
        self.todo = list(bit_order)
        self.rep_count = rep_count

    def advance(self, rep_index):
        if not self.todo:
            return
        bit = self.todo.pop(0)
        ax = self.axis_bits.index(bit)
        mine = (rep_index >> bit) & 1
        keep = lax.dynamic_index_in_dim(self.x, mine, ax, keepdims=False)
        send = lax.dynamic_index_in_dim(self.x, 1 - mine, ax, keepdims=False)
        pairs = [(i, i ^ (1 << bit)) for i in range(self.rep_count)]
        self.x = keep + lax.ppermute(send, "rep", perm=pairs)
        self.axis_bits.pop(ax)

    def result(self):
        return self.x.reshape(self.part, self.width)


class _Pair:
    def __init__(self, partial2, orders, rep_count):
        self.levels = rep_count.bit_length() - 1
        self.rep_count = rep_count
        self.part = partial2.shape[1] // rep_count
        self.width = partial2.shape[2]
        self.joint = partial2.reshape((2,) + (2,) * self.levels + (self.part, self.width))
        self.orders = orders
        self.halves = None

    @property
    def todo(self):
        return self.halves is None or any(h.todo for h in self.halves)

    @property
    def x(self):
        return self.joint if self.halves is None else [h.x for h in self.halves]

    @x.setter
    def x(self, value):
        if self.halves is None:
            self.joint = value
        else:
            for h, v in zip(self.halves, value):
                h.x = v

    def advance(self, rep_index):
        if self.halves is not None:
            for h in self.halves:
                h.advance(rep_index)
            return
        bit = self.orders[0][0]
        ax = 1 + (self.levels - 1 - bit)
        mine = (rep_index >> bit) & 1
        keep = lax.dynamic_index_in_dim(self.joint, mine, ax, keepdims=False)
        send = lax.dynamic_index_in_dim(self.joint, 1 - mine, ax, keepdims=False)
        pairs = [(i, i ^ (1 << bit)) for i in range(self.rep_count)]
        both = keep + lax.ppermute(send, "rep", perm=pairs)
        self.halves = []
        for h in range(2):
            flow = object.__new__(_Halving)
            flow.levels, flow.part, flow.width = self.levels, self.part, self.width
            flow.rep_count = self.rep_count
            flow.x = both[h]
            flow.axis_bits = [b for b in range(self.levels - 1, -1, -1) if b != bit]
            flow.todo = list(self.orders[h][1:])
            self.halves.append(flow)

    def result(self):
        return jnp.concatenate([h.result() for h in self.halves], axis=1)


def on_device(amplitudes, integrals, ab_list, cd_list, live_count):
    own_count = lax.axis_size("own")
    rep_count = lax.axis_size("rep")
    peer_count = own_count * rep_count
    slot_count = integrals.shape[0] // peer_count
    received = lax.all_to_all(integrals, ("own", "rep"), split_axis=0, concat_axis=0, tiled=True)
    ab_ids = ab_list.reshape(-1)
    cd_ids = cd_list.reshape(-1)
    live_mask = (
        jnp.arange(slot_count, dtype=jnp.int32)[None, :] < live_count.reshape(peer_count, 1)
    ).reshape(-1)
    order, starts = _slot_order(ab_ids, live_mask, AB_DEV)
    local_rows, width = amplitudes.shape
    subs = rep_count // own_count
    part = local_rows // (subs * N_CHUNK)
    local4 = amplitudes.reshape(subs, N_CHUNK, part, width)
    rep_index = lax.axis_index("rep")
    levels = rep_count.bit_length() - 1
    orders = (list(range(levels)), [0] + list(range(levels - 1, 0, -1)))
    gathered = [lax.all_gather(local4[:, c], "own", axis=0, tiled=True) for c in range(N_CHUNK)]
    flows = []
    for chunk in range(N_CHUNK):
        for flow in flows:
            flow.advance(rep_index)
        if flows:
            amp3, held = lax.optimization_barrier((gathered[chunk], [f.x for f in flows]))
            for flow, x in zip(flows, held):
                flow.x = x
        else:
            amp3 = gathered[chunk]
        partial = _ladder_products(amp3, received, order, starts, ab_ids, cd_ids, AB_DEV)
        flows.append(_Pair(partial, orders, rep_count))
    out = None
    while any(flow.todo for flow in flows):
        for flow in flows:
            flow.advance(rep_index)
        if out is None:
            out = jnp.zeros((N_CHUNK * part, width), jnp.float32)
        for c, flow in enumerate(flows):
            if not flow.todo and not getattr(flow, "placed", False):
                flow.placed = True
                out = lax.dynamic_update_slice(out, flow.result(), (c * part, 0))
    return out


def solution(mesh):
    return jax.shard_map(
        on_device,
        mesh=mesh,
        in_specs=(
            P("own", "rep"),
            P(("own", "rep"), None, None),
            P(("own", "rep"), None, None),
            P(("own", "rep"), None, None),
            P(("own", "rep"), None),
        ),
        out_specs=P("rep", "own"),
        check_vma=False,
    )
```

```python
import functools

import jax
import jax.numpy as jnp
from jax import lax
from jax.experimental import pallas as pl
from jax.experimental.pallas import tpu as pltpu
from jax.sharding import PartitionSpec as P

AB_DEV = 16
N_CHUNK = 4


def _slot_order(ab_ids, live_mask, ab_count):
    n = ab_ids.shape[0]
    key = jnp.where(live_mask, ab_ids, ab_count)
    idx = jnp.arange(n, dtype=jnp.int32)
    earlier = (key[None, :] < key[:, None]) | ((key[None, :] == key[:, None]) & (idx[None, :] < idx[:, None]))
    rank = jnp.sum(earlier.astype(jnp.int32), axis=1)
    order = jnp.sum(jnp.where(rank[None, :] == idx[:, None], idx[None, :], 0), axis=1).astype(jnp.int32)
    bounds = jnp.arange(ab_count + 1, dtype=jnp.int32)
    starts = jnp.sum((key[None, :] < bounds[:, None]).astype(jnp.int32), axis=1).astype(jnp.int32)
    return order, starts


def _ladder_kernel(order_ref, starts_ref, ab_ref, cd_ref, amp_ref, tiles_ref, out_ref, weight_ref):
    step = pl.program_id(0)
    tile = tiles_ref.shape[-1]
    groups, part, width = amp_ref.shape
    per_step = out_ref.shape[-1] // tile
    first = step * per_step

    @pl.when(step == 0)
    def _():
        weight_ref[...] = jnp.zeros(weight_ref.shape, weight_ref.dtype)

    def place(t, carry, clear=False):
        i = order_ref[t]
        row = pl.multiple_of(cd_ref[i] * tile, tile)
        col = pl.multiple_of((ab_ref[i] - first) * tile, tile)
        block = jnp.zeros((tile, tile), weight_ref.dtype) if clear else tiles_ref[i]
        weight_ref[pl.ds(row, tile), pl.ds(col, tile)] = block
        return carry

    lax.fori_loop(starts_ref[first], starts_ref[first + per_step], place, 0)
    lhs = amp_ref[...].reshape(groups * part, width)
    out_ref[...] = jnp.dot(lhs, weight_ref[...], preferred_element_type=jnp.float32)
    lax.fori_loop(
        starts_ref[first], starts_ref[first + per_step], lambda t, c: place(t, c, clear=True), 0
    )


def _ladder_products(amp3, tiles, order, starts, ab_ids, cd_ids, ab_count):
    groups, part, width = amp3.shape
    rows = groups * part
    n, tile, _ = tiles.shape
    per_step = ab_count // 2 if ab_count % 2 == 0 else 1
    steps_per_half = ab_count // (2 * per_step)
    cost = pl.CostEstimate(
        flops=2 * rows * width * ab_count * tile,
        transcendentals=0,
        bytes_accessed=rows * width * 2 + tiles.size * 2 + rows * ab_count * tile * 4,
    )
    grid_spec = pltpu.PrefetchScalarGridSpec(
        num_scalar_prefetch=4,
        grid=(ab_count // per_step,),
        in_specs=[
            pl.BlockSpec((groups, part, width), lambda j, *_: (0, 0, 0)),
            pl.BlockSpec((n, tile, tile), lambda j, *_: (0, 0, 0)),
        ],
        out_specs=pl.BlockSpec(
            (None, rows, per_step * tile), lambda j, *_: (j // steps_per_half, 0, j % steps_per_half)
        ),
        scratch_shapes=[pltpu.VMEM((width, per_step * tile), tiles.dtype)],
    )
    return pl.pallas_call(
        _ladder_kernel,
        grid_spec=grid_spec,
        out_shape=jax.ShapeDtypeStruct((2, rows, ab_count * tile // 2), jnp.float32),
        cost_estimate=cost,
    )(order, starts, ab_ids, cd_ids, amp3, tiles)


class _Halving:
    def __init__(self, partial, bit_order, rep_count):
        self.levels = rep_count.bit_length() - 1
        self.part = partial.shape[0] // rep_count
        self.width = partial.shape[-1]
        self.x = partial.reshape((2,) * self.levels + (self.part, self.width))
        self.axis_bits = list(range(self.levels - 1, -1, -1))
        self.todo = list(bit_order)
        self.rep_count = rep_count

    def advance(self, rep_index):
        if not self.todo:
            return
        bit = self.todo.pop(0)
        ax = self.axis_bits.index(bit)
        mine = (rep_index >> bit) & 1
        keep = lax.dynamic_index_in_dim(self.x, mine, ax, keepdims=False)
        send = lax.dynamic_index_in_dim(self.x, 1 - mine, ax, keepdims=False)
        pairs = [(i, i ^ (1 << bit)) for i in range(self.rep_count)]
        self.x = keep + lax.ppermute(send, "rep", perm=pairs)
        self.axis_bits.pop(ax)

    def result(self):
        return self.x.reshape(self.part, self.width)


class _Pair:
    def __init__(self, partial2, orders, rep_count):
        self.levels = rep_count.bit_length() - 1
        self.rep_count = rep_count
        self.part = partial2.shape[1] // rep_count
        self.width = partial2.shape[2]
        self.joint = partial2.reshape((2,) + (2,) * self.levels + (self.part, self.width))
        self.orders = orders
        self.halves = None

    @property
    def todo(self):
        return self.halves is None or any(h.todo for h in self.halves)

    @property
    def x(self):
        return self.joint if self.halves is None else [h.x for h in self.halves]

    @x.setter
    def x(self, value):
        if self.halves is None:
            self.joint = value
        else:
            for h, v in zip(self.halves, value):
                h.x = v

    def advance(self, rep_index):
        if self.halves is not None:
            for h in self.halves:
                h.advance(rep_index)
            return
        bit = self.orders[0][0]
        ax = 1 + (self.levels - 1 - bit)
        mine = (rep_index >> bit) & 1
        keep = lax.dynamic_index_in_dim(self.joint, mine, ax, keepdims=False)
        send = lax.dynamic_index_in_dim(self.joint, 1 - mine, ax, keepdims=False)
        pairs = [(i, i ^ (1 << bit)) for i in range(self.rep_count)]
        both = keep + lax.ppermute(send, "rep", perm=pairs)
        self.halves = []
        for h in range(2):
            flow = object.__new__(_Halving)
            flow.levels, flow.part, flow.width = self.levels, self.part, self.width
            flow.rep_count = self.rep_count
            flow.x = both[h]
            flow.axis_bits = [b for b in range(self.levels - 1, -1, -1) if b != bit]
            flow.todo = list(self.orders[h][1:])
            self.halves.append(flow)

    def result(self):
        return jnp.concatenate([h.result() for h in self.halves], axis=1)


def on_device(amplitudes, integrals, ab_list, cd_list, live_count):
    own_count = lax.axis_size("own")
    rep_count = lax.axis_size("rep")
    peer_count = own_count * rep_count
    slot_count = integrals.shape[0] // peer_count
    received = lax.all_to_all(integrals, ("own", "rep"), split_axis=0, concat_axis=0, tiled=True)
    ab_ids = ab_list.reshape(-1)
    cd_ids = cd_list.reshape(-1)
    live_mask = (
        jnp.arange(slot_count, dtype=jnp.int32)[None, :] < live_count.reshape(peer_count, 1)
    ).reshape(-1)
    order, starts = _slot_order(ab_ids, live_mask, AB_DEV)
    local_rows, width = amplitudes.shape
    subs = rep_count // own_count
    part = local_rows // (subs * N_CHUNK)
    local4 = amplitudes.reshape(subs, N_CHUNK, part, width)
    rep_index = lax.axis_index("rep")
    levels = rep_count.bit_length() - 1
    orders = (list(range(levels)), [0] + list(range(levels - 1, 0, -1)))
    gathered = [lax.all_gather(local4[:, c], "own", axis=0, tiled=True) for c in range(N_CHUNK)]
    flows = []
    for chunk in range(N_CHUNK):
        for flow in flows:
            flow.advance(rep_index)
        if flows:
            amp3, held = lax.optimization_barrier((gathered[chunk], [f.x for f in flows]))
            for flow, x in zip(flows, held):
                flow.x = x
        else:
            amp3 = gathered[chunk]
        partial = _ladder_products(amp3, received, order, starts, ab_ids, cd_ids, AB_DEV)
        flows.append(_Pair(partial, orders, rep_count))
    while any(flow.todo for flow in flows):
        for flow in flows:
            flow.advance(rep_index)
    pieces = [flow.result() for flow in flows]
    return jnp.concatenate(pieces, axis=0)


def solution(mesh):
    return jax.shard_map(
        on_device,
        mesh=mesh,
        in_specs=(
            P("own", "rep"),
            P(("own", "rep"), None, None),
            P(("own", "rep"), None, None),
            P(("own", "rep"), None, None),
            P(("own", "rep"), None),
        ),
        out_specs=P("rep", "own"),
        check_vma=False,
    )
```

```python
import functools

import jax
import jax.numpy as jnp
from jax import lax
from jax.experimental import pallas as pl
from jax.experimental.pallas import tpu as pltpu
from jax.sharding import PartitionSpec as P

AB_DEV = 16
N_CHUNK = 4


def _slot_order(ab_ids, live_mask, ab_count):
    n = ab_ids.shape[0]
    key = jnp.where(live_mask, ab_ids, ab_count)
    idx = jnp.arange(n, dtype=jnp.int32)
    earlier = (key[None, :] < key[:, None]) | ((key[None, :] == key[:, None]) & (idx[None, :] < idx[:, None]))
    rank = jnp.sum(earlier.astype(jnp.int32), axis=1)
    order = jnp.sum(jnp.where(rank[None, :] == idx[:, None], idx[None, :], 0), axis=1).astype(jnp.int32)
    bounds = jnp.arange(ab_count + 1, dtype=jnp.int32)
    starts = jnp.sum((key[None, :] < bounds[:, None]).astype(jnp.int32), axis=1).astype(jnp.int32)
    return order, starts


def _ladder_kernel(order_ref, starts_ref, ab_ref, cd_ref, amp_ref, tiles_ref, out_ref, weight_ref):
    step = pl.program_id(0)
    tile = tiles_ref.shape[-1]
    groups, part, width = amp_ref.shape
    per_step = out_ref.shape[-1] // tile
    first = step * per_step

    @pl.when(step == 0)
    def _():
        weight_ref[...] = jnp.zeros(weight_ref.shape, weight_ref.dtype)

    def place(t, carry, clear=False):
        i = order_ref[t]
        row = pl.multiple_of(cd_ref[i] * tile, tile)
        col = pl.multiple_of((ab_ref[i] - first) * tile, tile)
        block = jnp.zeros((tile, tile), weight_ref.dtype) if clear else tiles_ref[i]
        weight_ref[pl.ds(row, tile), pl.ds(col, tile)] = block
        return carry

    lax.fori_loop(starts_ref[first], starts_ref[first + per_step], place, 0)
    lhs = amp_ref[...].reshape(groups * part, width)
    out_ref[...] = jnp.dot(lhs, weight_ref[...], preferred_element_type=jnp.float32)
    lax.fori_loop(
        starts_ref[first], starts_ref[first + per_step], lambda t, c: place(t, c, clear=True), 0
    )


def _ladder_products(amp3, tiles, order, starts, ab_ids, cd_ids, ab_count):
    groups, part, width = amp3.shape
    rows = groups * part
    n, tile, _ = tiles.shape
    per_step = 4 if ab_count % 8 == 0 else 1
    steps_per_half = ab_count // (2 * per_step)
    cost = pl.CostEstimate(
        flops=2 * rows * width * ab_count * tile,
        transcendentals=0,
        bytes_accessed=rows * width * 2 + tiles.size * 2 + rows * ab_count * tile * 4,
    )
    grid_spec = pltpu.PrefetchScalarGridSpec(
        num_scalar_prefetch=4,
        grid=(ab_count // per_step,),
        in_specs=[
            pl.BlockSpec((groups, part, width), lambda j, *_: (0, 0, 0)),
            pl.BlockSpec((n, tile, tile), lambda j, *_: (0, 0, 0)),
        ],
        out_specs=pl.BlockSpec(
            (None, rows, per_step * tile), lambda j, *_: (j // steps_per_half, 0, j % steps_per_half)
        ),
        scratch_shapes=[pltpu.VMEM((width, per_step * tile), tiles.dtype)],
    )
    return pl.pallas_call(
        _ladder_kernel,
        grid_spec=grid_spec,
        out_shape=jax.ShapeDtypeStruct((2, rows, ab_count * tile // 2), jnp.float32),
        cost_estimate=cost,
    )(order, starts, ab_ids, cd_ids, amp3, tiles)


class _Halving:
    def __init__(self, partial, bit_order, rep_count):
        self.levels = rep_count.bit_length() - 1
        self.part = partial.shape[0] // rep_count
        self.width = partial.shape[-1]
        self.x = partial.reshape((2,) * self.levels + (self.part, self.width))
        self.axis_bits = list(range(self.levels - 1, -1, -1))
        self.todo = list(bit_order)
        self.rep_count = rep_count

    def advance(self, rep_index):
        if not self.todo:
            return
        bit = self.todo.pop(0)
        ax = self.axis_bits.index(bit)
        mine = (rep_index >> bit) & 1
        keep = lax.dynamic_index_in_dim(self.x, mine, ax, keepdims=False)
        send = lax.dynamic_index_in_dim(self.x, 1 - mine, ax, keepdims=False)
        pairs = [(i, i ^ (1 << bit)) for i in range(self.rep_count)]
        self.x = keep + lax.ppermute(send, "rep", perm=pairs)
        self.axis_bits.pop(ax)

    def result(self):
        return self.x.reshape(self.part, self.width)


class _Pair:
    def __init__(self, partial2, orders, rep_count):
        self.levels = rep_count.bit_length() - 1
        self.rep_count = rep_count
        self.part = partial2.shape[1] // rep_count
        self.width = partial2.shape[2]
        self.joint = partial2.reshape((2,) + (2,) * self.levels + (self.part, self.width))
        self.orders = orders
        self.halves = None

    @property
    def todo(self):
        return self.halves is None or any(h.todo for h in self.halves)

    @property
    def x(self):
        return self.joint if self.halves is None else [h.x for h in self.halves]

    @x.setter
    def x(self, value):
        if self.halves is None:
            self.joint = value
        else:
            for h, v in zip(self.halves, value):
                h.x = v

    def advance(self, rep_index):
        if self.halves is not None:
            for h in self.halves:
                h.advance(rep_index)
            return
        bit = self.orders[0][0]
        ax = 1 + (self.levels - 1 - bit)
        mine = (rep_index >> bit) & 1
        keep = lax.dynamic_index_in_dim(self.joint, mine, ax, keepdims=False)
        send = lax.dynamic_index_in_dim(self.joint, 1 - mine, ax, keepdims=False)
        pairs = [(i, i ^ (1 << bit)) for i in range(self.rep_count)]
        both = keep + lax.ppermute(send, "rep", perm=pairs)
        self.halves = []
        for h in range(2):
            flow = object.__new__(_Halving)
            flow.levels, flow.part, flow.width = self.levels, self.part, self.width
            flow.rep_count = self.rep_count
            flow.x = both[h]
            flow.axis_bits = [b for b in range(self.levels - 1, -1, -1) if b != bit]
            flow.todo = list(self.orders[h][1:])
            self.halves.append(flow)

    def result(self):
        return jnp.concatenate([h.result() for h in self.halves], axis=1)


def on_device(amplitudes, integrals, ab_list, cd_list, live_count):
    own_count = lax.axis_size("own")
    rep_count = lax.axis_size("rep")
    peer_count = own_count * rep_count
    slot_count = integrals.shape[0] // peer_count
    received = lax.all_to_all(integrals, ("own", "rep"), split_axis=0, concat_axis=0, tiled=True)
    ab_ids = ab_list.reshape(-1)
    cd_ids = cd_list.reshape(-1)
    live_mask = (
        jnp.arange(slot_count, dtype=jnp.int32)[None, :] < live_count.reshape(peer_count, 1)
    ).reshape(-1)
    order, starts = _slot_order(ab_ids, live_mask, AB_DEV)
    local_rows, width = amplitudes.shape
    subs = rep_count // own_count
    part = local_rows // (subs * N_CHUNK)
    local4 = amplitudes.reshape(subs, N_CHUNK, part, width)
    rep_index = lax.axis_index("rep")
    levels = rep_count.bit_length() - 1
    orders = (list(range(levels)), [0] + list(range(levels - 1, 0, -1)))
    gathered = [lax.all_gather(local4[:, c], "own", axis=0, tiled=True) for c in range(N_CHUNK)]
    flows = []
    for chunk in range(N_CHUNK):
        for flow in flows:
            flow.advance(rep_index)
        if flows:
            amp3, held = lax.optimization_barrier((gathered[chunk], [f.x for f in flows]))
            for flow, x in zip(flows, held):
                flow.x = x
        else:
            amp3 = gathered[chunk]
        partial = _ladder_products(amp3, received, order, starts, ab_ids, cd_ids, AB_DEV)
        flows.append(_Pair(partial, orders, rep_count))
    while any(flow.todo for flow in flows):
        for flow in flows:
            flow.advance(rep_index)
    pieces = [flow.result() for flow in flows]
    return jnp.concatenate(pieces, axis=0)


def solution(mesh):
    return jax.shard_map(
        on_device,
        mesh=mesh,
        in_specs=(
            P("own", "rep"),
            P(("own", "rep"), None, None),
            P(("own", "rep"), None, None),
            P(("own", "rep"), None, None),
            P(("own", "rep"), None),
        ),
        out_specs=P("rep", "own"),
        check_vma=False,
    )
```
